256 devices in a mesh: ctx: 64 (over y, z, core), head: 4 (over x).
Axes of the slice: x: 4, y: 4, z: 8, core: 2. Of those that a mesh axis runs over, the one named last changes fastest.
Arguments:
- queries: bfloat16 [8192, 4096], P('ctx', 'head'), may hold values from -6 to 6
- key_heads: bfloat16 [8192, 4096], P('ctx', 'head'), may hold values from -0.59765625 to 0.59765625
- value_heads: bfloat16 [8192, 4096], P('ctx', 'head'), may hold values from -12 to 12
- gate_logits: bfloat16 [8192, 4096], P('ctx', 'head'), may hold values from -9 to 9
- log_decay: float32 [8192, 32], P('ctx', 'head'), may hold values from -2 to 0
- attn_gain: float32 [4096], P('head'), may hold values from 0.25 to 1.75
- out_weight: bfloat16 [32, 128, 6144], P('head', 'ctx'), may hold values from -0.09375 to 0.09375
- residual: bfloat16 [8192, 6144], P('ctx'), may hold values from -24 to 24
- norm_gain: float32 [6144], replicated, may hold values from 0.25 to 1.75
- router_weight: bfloat16 [6144, 32], replicated, may hold values from -0.078125 to 0.078125
- expert_ids: int32 [8192, 2], P('ctx'), may hold values from 0 to 31, as said below
- expert_gate: bfloat16 [36864, 6144], P(('ctx', 'head')), may hold values from -0.078125 to 0.078125
- expert_up: bfloat16 [36864, 6144], P(('ctx', 'head')), may hold values from -0.078125 to 0.078125
- expert_down: bfloat16 [36864, 6144], P('ctx', 'head'), may hold values from -0.09375 to 0.09375
Outputs:
- layer_out: bfloat16 [8192, 6144], P('ctx', 'head')
The draws below stay inside these ranges and needn't reach their ends.
Inputs may be any that keep to these rules, and one draw needn't show every extreme that they name: `expert_ids`: A row's two ids differ; within the 128 rows of one block no id is named by more than 10 rows.
All inputs are finite; a program needn't handle non-finite values.
Results may differ from the reference program's by a relative error of at most 0.008.
Values may be sent and summed in bfloat16 or wider, within the bound.
No kernel may reach another device: no remote copies, remote signals or barrier semaphores. Data moves between devices by JAX's collectives and lax.ppermute only.
A program may use at most 128 MiB of HBM per device.

```python
import math
import jax
import jax.numpy as jnp
from jax import lax

D = 6144
HD = 128
H = 32
FF = 4608
EXPERTS = 32
EXP = 8
TOK_DEV = 128
MOST = 10
TOKENS = 8192
GROUP = 8
FF_ROW = 576


def draw_value_heads(key, part):
    subkeys = jax.random.split(key, 2)
    column_scale = jnp.exp(jax.random.uniform(subkeys[0], (H * HD,), jnp.float32, math.log(0.3), math.log(3.0)))
    base_values = jax.random.normal(subkeys[1], (TOKENS, H * HD), jnp.float32)
    return jnp.clip(base_values * column_scale[None, :], -12.0, 12.0).astype(jnp.bfloat16)


def draw_residual(key, part):
    subkeys = jax.random.split(key, 3)
    column_scale = jnp.exp(jax.random.uniform(subkeys[0], (1, D), jnp.float32, math.log(0.3), math.log(3.0)))
    row_scale = jnp.exp(jax.random.uniform(subkeys[1], (TOKENS, 1), jnp.float32, math.log(0.3), math.log(3.0)))
    base_values = jax.random.normal(subkeys[2], (TOKENS, D), jnp.float32)
    return jnp.clip(base_values * column_scale * row_scale, -24.0, 24.0).astype(jnp.bfloat16)


def draw_log_decay(key, part):
    subkeys = jax.random.split(key, 7)
    blocks = TOKENS // TOK_DEV
    fast_share = 0.5
    picker = jax.random.uniform(subkeys[0], (H,), jnp.float32)
    fast_rate = jax.random.uniform(subkeys[1], (H,), jnp.float32, 1.0 / 50.0, 1.0 / 30.0)
    slow_rate = jax.random.uniform(subkeys[2], (H,), jnp.float32, 0.03, 0.15) / TOKENS
    fading_rate_list = jnp.where(picker < fast_share, fast_rate, slow_rate)
    dispersion_extent = jnp.exp(jax.random.uniform(subkeys[3], (blocks, 1, H), jnp.float32, math.log(0.5), math.log(2.0)))
    dispersion_extent = jnp.broadcast_to(dispersion_extent, (blocks, TOK_DEV, H)).reshape(TOKENS, H)
    jitter_level = jax.random.uniform(subkeys[4], (TOKENS, H), jnp.float32, 0.5, 1.5)
    capacity_entries = jax.random.randint(subkeys[5], (3, H), 0, TOKENS)
    penalty_parts = jnp.log(jax.random.uniform(subkeys[6], (3, H), jnp.float32, 0.6, 0.8))
    sequence_offsets = jnp.arange(TOKENS)[:, None, None]
    expert_bundle_count = jnp.sum(jnp.where(sequence_offsets == capacity_entries[None, :, :], penalty_parts[None, :, :], 0.0), axis=1)
    return -fading_rate_list[None, :] * dispersion_extent * jitter_level + expert_bundle_count


def draw_expert_ids(key, part):
    subkeys = jax.random.split(key, 2)
    blocks = TOKENS // TOK_DEV
    full_expert = jax.random.randint(subkeys[0], (), 0, EXP)
    remaining = 2 * TOK_DEV - MOST
    expert_rank = jnp.arange(EXPERTS)
    counts = jnp.where(expert_rank == 0, MOST, jnp.clip(remaining - (expert_rank - 1) * MOST, 0, MOST))
    bounds = jnp.cumsum(counts)
    slot_index = jnp.arange(2 * TOK_DEV)
    owner_rank = jnp.sum((bounds[None, :] <= slot_index[:, None]).astype(jnp.int32), axis=1)

    def one_block(block_key):
        block_keys = jax.random.split(block_key, 3)
        others = jax.random.permutation(block_keys[0], EXPERTS - 1)
        expert_order = jnp.concatenate([full_expert[None], (full_expert + 1 + others) % EXPERTS])
        sequence = expert_order[owner_rank]
        row_pairs = sequence.reshape(2, TOK_DEV).T
        row_order = jax.random.permutation(block_keys[1], TOK_DEV)
        row_pairs = row_pairs[row_order]
        flip_bits = jax.random.randint(block_keys[2], (TOK_DEV, 1), 0, 2)
        return jnp.where(flip_bits == 1, row_pairs[:, ::-1], row_pairs)
    chosen_ids = jax.vmap(one_block)(jax.random.split(subkeys[1], blocks))
    return chosen_ids.reshape(TOKENS, 2).astype(jnp.int32)


def shard_levels(key, dims, cuts, low, largest):
    level = 1.0
    for axis_at, blocks in cuts:
        heights = jax.random.uniform(jax.random.fold_in(jax.random.fold_in(key, 6), axis_at), (blocks,), jnp.float32, low / len(cuts), largest / len(cuts))
        level = level * jnp.repeat(jnp.exp(heights), dims[axis_at] // blocks).reshape((-1,) + (1,) * (len(dims) - 1 - axis_at))
    return level


def centred(stream_key, extent, deviation, bound, cuts=(), held_as=jnp.bfloat16):
    drawn = deviation * jax.random.normal(stream_key, extent, jnp.float32)
    if cuts:
        drawn = drawn * shard_levels(stream_key, extent, cuts, -0.22, 0.18)
    return jnp.clip(drawn, -bound, bound).astype(held_as)


def setup_inputs(seed: int = 0) -> dict:
    key_of = jax.random.split(jax.random.key(seed), 15)
    queries = centred(key_of[0], (TOKENS, H * HD), 1.0, 6.0, ((0, 64), (1, 4)))
    key_heads = centred(key_of[1], (TOKENS, H * HD), 0.1, 0.59765625, ((0, 64), (1, 4)))
    value_heads = draw_value_heads(jax.random.fold_in(key_of[14], 71), 0)
    gate_logits = centred(key_of[3], (TOKENS, H * HD), 1.5, 9.0, ((0, 64), (1, 4)))
    log_decay = draw_log_decay(jax.random.fold_in(key_of[14], 71), 0)
    attn_gain = jnp.clip(1.0 + 0.15 * jax.random.normal(key_of[5], (H * HD,), jnp.float32), 0.25, 1.75)
    out_weight = centred(key_of[6], (H, HD, D), (H * HD) ** -0.5, 0.09375, ((0, 4), (1, 64)))
    residual = draw_residual(jax.random.fold_in(key_of[14], 71), 0)
    norm_gain = jnp.clip(1.0 + 0.15 * jax.random.normal(key_of[8], (D,), jnp.float32), 0.25, 1.75)
    router_weight = centred(key_of[9], (D, EXPERTS), D ** -0.5, 0.078125)
    expert_ids = draw_expert_ids(jax.random.fold_in(key_of[14], 71), 0)
    expert_gate = centred(key_of[11], (EXP * FF, D), D ** -0.5, 0.078125, ((0, 256),))
    expert_up = centred(key_of[12], (EXP * FF, D), D ** -0.5, 0.078125, ((0, 256),))
    expert_down = centred(key_of[13], (EXP * FF, D), FF ** -0.5, 0.09375, ((0, 64), (1, 4)))
    return {"queries": queries, "key_heads": key_heads, "value_heads": value_heads, "gate_logits": gate_logits, "log_decay": log_decay, "attn_gain": attn_gain, "out_weight": out_weight, "residual": residual, "norm_gain": norm_gain, "router_weight": router_weight, "expert_ids": expert_ids, "expert_gate": expert_gate, "expert_up": expert_up, "expert_down": expert_down}


epsilon = 1e-06
highest = lax.Precision.HIGHEST

def block_attention(carry_state, inputs):
    query_block, key_block, value_block, decay_block = inputs
    cumulative = jnp.cumsum(decay_block, axis=0)
    block_total = cumulative[-1]
    sequence_offsets = jnp.arange(TOK_DEV, dtype=jnp.int32)
    causal = (sequence_offsets[:, None] >= sequence_offsets[None, :])[:, :, None]
    decay_gaps = jnp.where(causal, cumulative[:, None, :] - cumulative[None, :, :], 0.0)
    scores = jnp.einsum('thd,shd->tsh', query_block.astype(jnp.float32), key_block.astype(jnp.float32))
    attn_probs = jnp.where(causal, scores * jnp.exp(decay_gaps), 0.0).astype(jnp.bfloat16)
    within = jnp.einsum('tsh,shd->thd', attn_probs.astype(jnp.float32), value_block.astype(jnp.float32))
    carried = jnp.einsum('thd,hde->the', query_block.astype(jnp.float32), carry_state, precision=highest)
    carried = carried * jnp.exp(cumulative)[:, :, None]
    keys_decayed = (key_block.astype(jnp.float32) * jnp.exp(block_total[None, :] - cumulative)[:, :, None]).astype(jnp.bfloat16)
    local_state = jnp.einsum('thd,the->hde', keys_decayed.astype(jnp.float32), value_block.astype(jnp.float32))
    next_state = jnp.exp(block_total)[:, None, None] * carry_state + local_state
    return (next_state, within + carried)

def run_expert(operands):
    buffer_rows, gate_rows, up_rows, down_rows = operands
    flat_rows = buffer_rows.reshape(-1, D)
    gate_part = jnp.dot(flat_rows, gate_rows.T, preferred_element_type=jnp.float32)
    up_part = jnp.dot(flat_rows, up_rows.T, preferred_element_type=jnp.float32)
    hidden_units = (jax.nn.silu(gate_part) * up_part).astype(jnp.bfloat16)
    summed = jnp.zeros((flat_rows.shape[0], D), jnp.float32)
    for member in range(GROUP):
        partial_value = jnp.dot(hidden_units[:, member * FF_ROW:(member + 1) * FF_ROW], down_rows[member * FF_ROW:(member + 1) * FF_ROW], preferred_element_type=jnp.float32).astype(jnp.bfloat16)
        summed = summed + partial_value.astype(jnp.float32)
    return summed.reshape(buffer_rows.shape)

def reference(queries, key_heads, value_heads, gate_logits, log_decay, attn_gain, out_weight, residual, norm_gain, router_weight, expert_ids, expert_gate, expert_up, expert_down):
    blocks = TOKENS // TOK_DEV
    query_blocks = queries.reshape(blocks, TOK_DEV, H, HD)
    key_blocks = key_heads.reshape(blocks, TOK_DEV, H, HD)
    value_blocks = value_heads.reshape(blocks, TOK_DEV, H, HD)
    decay_blocks = log_decay.reshape(blocks, TOK_DEV, H)
    zero_state = jnp.zeros((H, HD, HD), jnp.float32)
    _, attended = lax.scan(block_attention, zero_state, (query_blocks, key_blocks, value_blocks, decay_blocks))
    attended = attended.reshape(TOKENS, H, HD)
    rms_scale = lax.rsqrt(lax.optimization_barrier(jnp.mean(attended * attended, axis=-1, keepdims=True)) + epsilon)
    gate_open = jax.nn.sigmoid(gate_logits.astype(jnp.float32).reshape(TOKENS, H, HD))
    attn_mixed = (attended * rms_scale * attn_gain.reshape(H, HD) * gate_open).astype(jnp.bfloat16)
    projected = jnp.dot(attn_mixed.reshape(TOKENS, H * HD), out_weight.reshape(H * HD, D), preferred_element_type=jnp.float32)
    hidden_state = residual.astype(jnp.float32) + projected
    normed = (hidden_state * lax.rsqrt(lax.optimization_barrier(jnp.mean(hidden_state * hidden_state, axis=-1, keepdims=True)) + epsilon) * norm_gain).astype(jnp.bfloat16)
    logits = jnp.dot(normed, router_weight, preferred_element_type=jnp.float32)
    columns = jnp.arange(EXPERTS, dtype=jnp.int32)
    picked = lax.optimization_barrier(jnp.sum(jnp.where(columns[None, None, :] == expert_ids[:, :, None], logits[:, None, :], 0.0), axis=-1))
    route_gates = jax.nn.sigmoid(picked - picked[:, ::-1])
    route_ids = expert_ids.reshape(blocks, 2 * TOK_DEV).astype(jnp.int32)
    inside = route_ids < EXP
    onehot = (route_ids[:, :, None] == jnp.arange(EXP, dtype=jnp.int32)[None, None, :]).astype(jnp.int32)
    before = (jnp.cumsum(onehot, axis=1) - onehot).astype(jnp.int32)
    slot_index = lax.optimization_barrier(jnp.sum(before * onehot, axis=-1)).astype(jnp.int32)
    target = jnp.where(inside, route_ids, EXP).astype(jnp.int32)
    block_index = jnp.broadcast_to(jnp.arange(blocks, dtype=jnp.int32)[:, None], (blocks, 2 * TOK_DEV)).astype(jnp.int32)
    route_rows = jnp.repeat(normed.reshape(blocks, TOK_DEV, D), 2, axis=1)
    buffers = jnp.zeros((EXP, blocks, MOST, D), jnp.bfloat16).at[target, block_index, slot_index].set(route_rows, mode='drop')
    outputs = lax.map(run_expert, (buffers, expert_gate.reshape(EXP, FF, D), expert_up.reshape(EXP, FF, D), expert_down.reshape(EXP, FF, D)))
    safe_target = jnp.minimum(target, EXP - 1).astype(jnp.int32)
    fetched = outputs[safe_target, block_index, slot_index]
    weights = jnp.where(inside, route_gates.reshape(blocks, 2 * TOK_DEV), 0.0)
    mixture = lax.optimization_barrier(jnp.sum((fetched * weights[:, :, None]).reshape(blocks, TOK_DEV, 2, D), axis=2)).reshape(TOKENS, D)
    return (hidden_state + mixture).astype(jnp.bfloat16)
```

```python
import jax
import jax.numpy as jnp
from jax import lax
from jax.sharding import Mesh, PartitionSpec as P

EXP = 8
MOST = 10


epsilon = 1e-06
highest = lax.Precision.HIGHEST


def chain_weights(factors, target):
    count = factors.shape[0]
    index = jnp.arange(count)
    inside = (index[:, None] < index[None, :]) & (index[None, :] < target)
    spans = jnp.prod(jnp.where(inside[:, :, None], factors[None, :, :], 1.0), axis=1)
    return jnp.where((index < target)[:, None], spans, 0.0)


def pack_state(factor, state):
    heads, dim, _ = state.shape
    extra = jnp.broadcast_to(factor[:, None, None], (heads, 8, dim))
    return jnp.concatenate([state, extra], axis=1).astype(jnp.bfloat16)


def unpack_state(packed):
    dim = packed.shape[-1]
    return packed[..., dim, 0].astype(jnp.float32), packed[..., :dim, :].astype(jnp.float32)


def group_scan(factor, state, axis):
    place = lax.axis_index(axis)
    count = lax.axis_size(axis)
    factors, states = unpack_state(lax.all_gather(pack_state(factor, state), axis))
    into = chain_weights(factors, place)
    entering = jnp.einsum("kh,khde->hde", into, states, precision=highest)
    whole = chain_weights(factors, count)
    total_state = jnp.einsum("kh,khde->hde", whole, states, precision=highest)
    index = jnp.arange(count)
    before = jnp.prod(jnp.where((index < place)[:, None], factors, 1.0), axis=0)
    total_factor = jnp.prod(factors, axis=0)
    return before, entering, total_factor, total_state


def body(
    queries,
    key_heads,
    value_heads,
    gate_logits,
    log_decay,
    attn_gain,
    out_weight,
    residual,
    norm_gain,
    router_weight,
    expert_ids,
    expert_gate,
    expert_up,
    expert_down,
):
    ctx_count = lax.axis_size(("g", "j"))
    head_count = lax.axis_size("head")
    head_index = lax.axis_index("head")
    tok_rows = queries.shape[0]
    local_heads = log_decay.shape[1]
    head_dim = queries.shape[1] // local_heads
    model_width = residual.shape[1]
    share_width = model_width // head_count
    query_blocks = queries.reshape(tok_rows, local_heads, head_dim)
    key_blocks = key_heads.reshape(tok_rows, local_heads, head_dim)
    value_blocks = value_heads.reshape(tok_rows, local_heads, head_dim)
    cumulative = jnp.cumsum(log_decay, axis=0)
    block_total = cumulative[-1]
    keys_decayed = (
        key_blocks.astype(jnp.float32) * jnp.exp(block_total[None, :] - cumulative)[:, :, None]
    ).astype(jnp.bfloat16)
    local_state = jnp.einsum(
        "thd,the->hde", keys_decayed, value_blocks, preferred_element_type=jnp.float32
    )
    before, inner_entering, group_factor, group_state = group_scan(
        jnp.exp(block_total), local_state, "j"
    )
    _, outer_entering, _, _ = group_scan(group_factor, group_state, "g")
    entering = before[:, None, None] * outer_entering + inner_entering
    sequence_offsets = jnp.arange(tok_rows)
    causal = (sequence_offsets[:, None] >= sequence_offsets[None, :])[None, :, :]
    cum_heads = cumulative.T
    decay_gaps = jnp.where(causal, cum_heads[:, :, None] - cum_heads[:, None, :], 0.0)
    scores = jnp.einsum(
        "thd,shd->hts", query_blocks, key_blocks, preferred_element_type=jnp.float32
    )
    attn_probs = jnp.where(causal, scores * jnp.exp(decay_gaps), 0.0).astype(jnp.bfloat16)
    within = jnp.einsum(
        "hts,shd->thd", attn_probs, value_blocks, preferred_element_type=jnp.float32
    )
    carried = jnp.einsum(
        "thd,hde->the", query_blocks.astype(jnp.float32), entering, precision=highest
    )
    attended = within + carried * jnp.exp(cumulative)[:, :, None]
    rms_scale = lax.rsqrt(jnp.mean(attended * attended, axis=-1, keepdims=True) + epsilon)
    gate_open = jax.nn.sigmoid(
        gate_logits.astype(jnp.float32).reshape(tok_rows, local_heads, head_dim)
    )
    attn_mixed = (
        attended * rms_scale * attn_gain.reshape(local_heads, head_dim) * gate_open
    ).astype(jnp.bfloat16)
    row_whole = lax.all_gather(out_weight, ("g", "j"), axis=1, tiled=True)
    partial_sum = jnp.einsum(
        "thr,hrd->td", attn_mixed, row_whole, preferred_element_type=jnp.float32
    )
    projected = lax.psum(partial_sum.astype(jnp.bfloat16), "head").astype(jnp.float32)
    hidden_full = residual.astype(jnp.float32) + projected
    normed_full = (
        hidden_full
        * lax.rsqrt(jnp.mean(hidden_full * hidden_full, axis=-1, keepdims=True) + epsilon)
        * norm_gain[None, :]
    ).astype(jnp.bfloat16)
    hidden_share = lax.dynamic_slice_in_dim(hidden_full, head_index * share_width, share_width, 1)
    logits = jnp.dot(normed_full, router_weight, preferred_element_type=jnp.float32)
    columns = jnp.arange(router_weight.shape[1], dtype=jnp.int32)
    picked = jnp.sum(
        jnp.where(columns[None, None, :] == expert_ids[:, :, None], logits[:, None, :], 0.0),
        axis=-1,
    )
    route_gates = jax.nn.sigmoid(picked - picked[:, ::-1])
    route_ids = expert_ids.reshape(-1)
    onehot = (route_ids[:, None] == jnp.arange(EXP, dtype=jnp.int32)[None, :]).astype(jnp.int32)
    before_count = jnp.cumsum(onehot, axis=0) - onehot
    slot_index = jnp.sum(before_count * onehot, axis=1)
    slot_range = jnp.arange(MOST, dtype=jnp.int32)
    placed = (onehot.T[:, None, :] == 1) & (slot_index[None, None, :] == slot_range[None, :, None])
    chooser = (
        jnp.sum(placed.reshape(EXP, MOST, tok_rows, 2).astype(jnp.float32), axis=3)
        .astype(jnp.bfloat16)
        .reshape(EXP * MOST, tok_rows)
    )
    weighted = jnp.sum(
        (placed.astype(jnp.float32) * route_gates.reshape(-1)[None, None, :]).reshape(
            EXP, MOST, tok_rows, 2
        ),
        axis=3,
    )
    group = ctx_count // EXP
    packed = (
        jnp.dot(chooser, normed_full, preferred_element_type=jnp.float32)
        .astype(jnp.bfloat16)
        .reshape(EXP, MOST, model_width)
    )
    by_group = lax.all_to_all(packed, "g", split_axis=0, concat_axis=0, tiled=True)
    arrived = lax.all_gather(by_group, "j", axis=1, tiled=False)
    sources = arrived.shape[0] * arrived.shape[1]
    slots_now = arrived.shape[2]
    flat_rows = arrived.reshape(sources * slots_now, model_width)
    gate_part = jnp.einsum("rd,fd->rf", flat_rows, expert_gate, preferred_element_type=jnp.float32)
    up_part = jnp.einsum("rd,fd->rf", flat_rows, expert_up, preferred_element_type=jnp.float32)
    hidden_units = (
        (jax.nn.silu(gate_part) * up_part).astype(jnp.bfloat16).reshape(sources, slots_now, -1)
    )
    joined = lax.all_gather(hidden_units, "head", axis=2, tiled=True)
    partial_value = jnp.einsum(
        "nmf,fd->nmd", joined, expert_down, preferred_element_type=jnp.float32
    ).astype(jnp.bfloat16)
    returned = lax.all_to_all(partial_value, ("g", "j"), split_axis=0, concat_axis=0, tiled=True)
    summed = jnp.sum(returned.astype(jnp.float32).reshape(EXP, group, MOST, share_width), axis=1)
    mixture = jnp.einsum("est,esd->td", weighted, summed, precision=highest)
    return (hidden_share + mixture).astype(jnp.bfloat16)


def solution(mesh):
    ctx_count = mesh.shape["ctx"]
    head_count = mesh.shape["head"]
    split = Mesh(
        mesh.devices.reshape(EXP, ctx_count // EXP, head_count), ("g", "j", "head")
    )
    ctx = ("g", "j")
    return jax.shard_map(
        body,
        mesh=split,
        in_specs=(
            P(ctx, "head"),
            P(ctx, "head"),
            P(ctx, "head"),
            P(ctx, "head"),
            P(ctx, "head"),
            P("head"),
            P("head", ctx, None),
            P(ctx, None),
            P(),
            P(),
            P(ctx, None),
            P(("g", "j", "head"), None),
            P(("g", "j", "head"), None),
            P(ctx, "head"),
        ),
        out_specs=P(ctx, "head"),
        check_vma=False,
    )
```

```python
import jax
import jax.numpy as jnp
from jax import lax
from jax.sharding import Mesh, PartitionSpec as P

EXP = 8
MOST = 10


epsilon = 1e-06
highest = lax.Precision.HIGHEST


def pack_state(factor, state):
    heads, dim, _ = state.shape
    extra = jnp.broadcast_to(factor[:, None, None], (heads, 8, dim))
    return jnp.concatenate([state, extra], axis=1)


def unpack_state(packed):
    dim = packed.shape[-1]
    return packed[:, dim, 0], packed[:, :dim, :]


def prefix_scan(factor, state, axis, count):
    place = lax.axis_index(axis)

    def shift(value, distance):
        return lax.ppermute(value, axis, [(i, i + distance) for i in range(count - distance)])

    identity = pack_state(jnp.ones_like(factor), jnp.zeros_like(state))
    current = jnp.where(place >= 1, shift(pack_state(factor, state), 1), identity)
    distance = 1
    while distance < count:
        earlier_factor, earlier_state = unpack_state(shift(current, distance))
        later_factor, later_state = unpack_state(current)
        joined = pack_state(
            earlier_factor * later_factor,
            later_factor[:, None, None] * earlier_state + later_state,
        )
        current = jnp.where(place >= distance, joined, current)
        distance *= 2
    return unpack_state(current)[1]


def body(
    queries,
    key_heads,
    value_heads,
    gate_logits,
    log_decay,
    attn_gain,
    out_weight,
    residual,
    norm_gain,
    router_weight,
    expert_ids,
    expert_gate,
    expert_up,
    expert_down,
):
    ctx_count = lax.axis_size(("g", "j"))
    head_count = lax.axis_size("head")
    head_index = lax.axis_index("head")
    tok_rows = queries.shape[0]
    local_heads = log_decay.shape[1]
    head_dim = queries.shape[1] // local_heads
    model_width = residual.shape[1]
    share_width = model_width // head_count
    query_blocks = queries.reshape(tok_rows, local_heads, head_dim)
    key_blocks = key_heads.reshape(tok_rows, local_heads, head_dim)
    value_blocks = value_heads.reshape(tok_rows, local_heads, head_dim)
    cumulative = jnp.cumsum(log_decay, axis=0)
    block_total = cumulative[-1]
    keys_decayed = (
        key_blocks.astype(jnp.float32) * jnp.exp(block_total[None, :] - cumulative)[:, :, None]
    ).astype(jnp.bfloat16)
    local_state = jnp.einsum(
        "thd,the->hde", keys_decayed, value_blocks, preferred_element_type=jnp.float32
    )
    entering = prefix_scan(jnp.exp(block_total), local_state, ("g", "j"), ctx_count)
    sequence_offsets = jnp.arange(tok_rows)
    causal = (sequence_offsets[:, None] >= sequence_offsets[None, :])[None, :, :]
    cum_heads = cumulative.T
    decay_gaps = jnp.where(causal, cum_heads[:, :, None] - cum_heads[:, None, :], 0.0)
    scores = jnp.einsum(
        "thd,shd->hts", query_blocks, key_blocks, preferred_element_type=jnp.float32
    )
    attn_probs = jnp.where(causal, scores * jnp.exp(decay_gaps), 0.0).astype(jnp.bfloat16)
    within = jnp.einsum(
        "hts,shd->thd", attn_probs, value_blocks, preferred_element_type=jnp.float32
    )
    carried = jnp.einsum(
        "thd,hde->the", query_blocks.astype(jnp.float32), entering, precision=highest
    )
    attended = within + carried * jnp.exp(cumulative)[:, :, None]
    rms_scale = lax.rsqrt(jnp.mean(attended * attended, axis=-1, keepdims=True) + epsilon)
    gate_open = jax.nn.sigmoid(
        gate_logits.astype(jnp.float32).reshape(tok_rows, local_heads, head_dim)
    )
    attn_mixed = (
        attended * rms_scale * attn_gain.reshape(local_heads, head_dim) * gate_open
    ).astype(jnp.bfloat16)
    row_whole = lax.all_gather(out_weight, ("g", "j"), axis=1, tiled=True)
    partial_sum = jnp.einsum(
        "thr,hrd->td", attn_mixed, row_whole, preferred_element_type=jnp.float32
    )
    projected = lax.psum(partial_sum.astype(jnp.bfloat16), "head").astype(jnp.float32)
    hidden_full = residual.astype(jnp.float32) + projected
    normed_full = (
        hidden_full
        * lax.rsqrt(jnp.mean(hidden_full * hidden_full, axis=-1, keepdims=True) + epsilon)
        * norm_gain[None, :]
    ).astype(jnp.bfloat16)
    hidden_share = lax.dynamic_slice_in_dim(hidden_full, head_index * share_width, share_width, 1)
    logits = jnp.dot(normed_full, router_weight, preferred_element_type=jnp.float32)
    columns = jnp.arange(router_weight.shape[1], dtype=jnp.int32)
    picked = jnp.sum(
        jnp.where(columns[None, None, :] == expert_ids[:, :, None], logits[:, None, :], 0.0),
        axis=-1,
    )
    route_gates = jax.nn.sigmoid(picked - picked[:, ::-1])
    route_ids = expert_ids.reshape(-1)
    onehot = (route_ids[:, None] == jnp.arange(EXP, dtype=jnp.int32)[None, :]).astype(jnp.int32)
    before_count = jnp.cumsum(onehot, axis=0) - onehot
    slot_index = jnp.sum(before_count * onehot, axis=1)
    slot_range = jnp.arange(MOST, dtype=jnp.int32)
    placed = (onehot.T[:, None, :] == 1) & (slot_index[None, None, :] == slot_range[None, :, None])
    chooser = (
        jnp.sum(placed.reshape(EXP, MOST, tok_rows, 2).astype(jnp.float32), axis=3)
        .astype(jnp.bfloat16)
        .reshape(EXP * MOST, tok_rows)
    )
    weighted = jnp.sum(
        (placed.astype(jnp.float32) * route_gates.reshape(-1)[None, None, :]).reshape(
            EXP, MOST, tok_rows, 2
        ),
        axis=3,
    )
    group = ctx_count // EXP
    packed = (
        jnp.dot(chooser, normed_full, preferred_element_type=jnp.float32)
        .astype(jnp.bfloat16)
        .reshape(EXP, MOST, model_width)
    )
    by_group = lax.all_to_all(packed, "g", split_axis=0, concat_axis=0, tiled=True)
    arrived = lax.all_gather(by_group, "j", axis=1, tiled=False)
    sources = arrived.shape[0] * arrived.shape[1]
    slots_now = arrived.shape[2]
    flat_rows = arrived.reshape(sources * slots_now, model_width)
    gate_part = jnp.einsum("rd,fd->rf", flat_rows, expert_gate, preferred_element_type=jnp.float32)
    up_part = jnp.einsum("rd,fd->rf", flat_rows, expert_up, preferred_element_type=jnp.float32)
    hidden_units = (
        (jax.nn.silu(gate_part) * up_part).astype(jnp.bfloat16).reshape(sources, slots_now, -1)
    )
    joined = lax.all_gather(hidden_units, "head", axis=2, tiled=True)
    partial_value = jnp.einsum(
        "nmf,fd->nmd", joined, expert_down, preferred_element_type=jnp.float32
    ).astype(jnp.bfloat16)
    returned = lax.all_to_all(partial_value, ("g", "j"), split_axis=0, concat_axis=0, tiled=True)
    summed = jnp.sum(returned.astype(jnp.float32).reshape(EXP, group, MOST, share_width), axis=1)
    mixture = jnp.einsum("est,esd->td", weighted, summed, precision=highest)
    return (hidden_share + mixture).astype(jnp.bfloat16)


def solution(mesh):
    ctx_count = mesh.shape["ctx"]
    head_count = mesh.shape["head"]
    split = Mesh(
        mesh.devices.reshape(EXP, ctx_count // EXP, head_count), ("g", "j", "head")
    )
    ctx = ("g", "j")
    return jax.shard_map(
        body,
        mesh=split,
        in_specs=(
            P(ctx, "head"),
            P(ctx, "head"),
            P(ctx, "head"),
            P(ctx, "head"),
            P(ctx, "head"),
            P("head"),
            P("head", ctx, None),
            P(ctx, None),
            P(),
            P(),
            P(ctx, None),
            P(("g", "j", "head"), None),
            P(("g", "j", "head"), None),
            P(ctx, "head"),
        ),
        out_specs=P(ctx, "head"),
        check_vma=False,
    )
```

```python
import jax
import jax.numpy as jnp
from jax import lax
from jax.sharding import Mesh, PartitionSpec as P

EXP = 8
MOST = 10


epsilon = 1e-06
highest = lax.Precision.HIGHEST


def pack_state(factor, state):
    heads, dim, _ = state.shape
    extra = jnp.broadcast_to(factor[:, None, None], (heads, 8, dim))
    return jnp.concatenate([state, extra], axis=1)


def unpack_state(packed):
    dim = packed.shape[-1]
    return packed[:, dim, 0], packed[:, :dim, :]


def prefix_scan(factor, state, axis, count):
    place = lax.axis_index(axis)

    def shift(value, distance):
        return lax.ppermute(value, axis, [(i, i + distance) for i in range(count - distance)])

    identity = pack_state(jnp.ones_like(factor), jnp.zeros_like(state))
    current = jnp.where(place >= 1, shift(pack_state(factor, state), 1), identity)
    distance = 1
    while distance < count:
        earlier_factor, earlier_state = unpack_state(shift(current, distance))
        later_factor, later_state = unpack_state(current)
        joined = pack_state(
            earlier_factor * later_factor,
            later_factor[:, None, None] * earlier_state + later_state,
        )
        current = jnp.where(place >= distance, joined, current)
        distance *= 2
    return unpack_state(current)[1]


def body(
    queries,
    key_heads,
    value_heads,
    gate_logits,
    log_decay,
    attn_gain,
    out_weight,
    residual,
    norm_gain,
    router_weight,
    expert_ids,
    expert_gate,
    expert_up,
    expert_down,
):
    ctx_count = lax.axis_size(("g", "j"))
    head_count = lax.axis_size("head")
    head_index = lax.axis_index("head")
    tok_rows = queries.shape[0]
    local_heads = log_decay.shape[1]
    head_dim = queries.shape[1] // local_heads
    model_width = residual.shape[1]
    share_width = model_width // head_count
    query_blocks = queries.reshape(tok_rows, local_heads, head_dim)
    key_blocks = key_heads.reshape(tok_rows, local_heads, head_dim)
    value_blocks = value_heads.reshape(tok_rows, local_heads, head_dim)
    cumulative = jnp.cumsum(log_decay, axis=0)
    block_total = cumulative[-1]
    keys_decayed = (
        key_blocks.astype(jnp.float32) * jnp.exp(block_total[None, :] - cumulative)[:, :, None]
    ).astype(jnp.bfloat16)
    local_state = jnp.einsum(
        "thd,the->hde", keys_decayed, value_blocks, preferred_element_type=jnp.float32
    )
    entering = prefix_scan(jnp.exp(block_total), local_state, ("g", "j"), ctx_count)
    sequence_offsets = jnp.arange(tok_rows)
    causal = (sequence_offsets[:, None] >= sequence_offsets[None, :])[None, :, :]
    cum_heads = cumulative.T
    decay_gaps = jnp.where(causal, cum_heads[:, :, None] - cum_heads[:, None, :], 0.0)
    scores = jnp.einsum(
        "thd,shd->hts", query_blocks, key_blocks, preferred_element_type=jnp.float32
    )
    attn_probs = jnp.where(causal, scores * jnp.exp(decay_gaps), 0.0).astype(jnp.bfloat16)
    within = jnp.einsum(
        "hts,shd->thd", attn_probs, value_blocks, preferred_element_type=jnp.float32
    )
    carried = jnp.einsum(
        "thd,hde->the", query_blocks.astype(jnp.float32), entering, precision=highest
    )
    attended = within + carried * jnp.exp(cumulative)[:, :, None]
    rms_scale = lax.rsqrt(jnp.mean(attended * attended, axis=-1, keepdims=True) + epsilon)
    gate_open = jax.nn.sigmoid(
        gate_logits.astype(jnp.float32).reshape(tok_rows, local_heads, head_dim)
    )
    attn_mixed = (
        attended * rms_scale * attn_gain.reshape(local_heads, head_dim) * gate_open
    ).astype(jnp.bfloat16)
    row_whole = lax.all_gather(out_weight, ("g", "j"), axis=1, tiled=True)
    partial_sum = jnp.einsum(
        "thr,hrd->td", attn_mixed, row_whole, preferred_element_type=jnp.float32
    )
    projected = lax.psum_scatter(
        partial_sum.astype(jnp.bfloat16), "head", scatter_dimension=1, tiled=True
    ).astype(jnp.float32)
    share_start = head_index * share_width
    residual_share = lax.dynamic_slice_in_dim(residual, share_start, share_width, 1)
    gain_share = lax.dynamic_slice_in_dim(norm_gain, share_start, share_width, 0)
    router_share = lax.dynamic_slice_in_dim(router_weight, share_start, share_width, 0)
    hidden_share = residual_share.astype(jnp.float32) + projected
    router_part = jnp.dot(
        hidden_share * gain_share[None, :],
        router_share.astype(jnp.float32),
        precision=highest,
    )
    square_part = jnp.sum(hidden_share * hidden_share, axis=-1, keepdims=True)
    stats = lax.psum(jnp.concatenate([square_part, router_part], axis=1), "head")
    row_scale = lax.rsqrt(stats[:, :1] / model_width + epsilon)
    logits = stats[:, 1:] * row_scale
    normed_share = (hidden_share * row_scale * gain_share[None, :]).astype(jnp.bfloat16)
    columns = jnp.arange(router_weight.shape[1], dtype=jnp.int32)
    picked = jnp.sum(
        jnp.where(columns[None, None, :] == expert_ids[:, :, None], logits[:, None, :], 0.0),
        axis=-1,
    )
    route_gates = jax.nn.sigmoid(picked - picked[:, ::-1])
    route_ids = expert_ids.reshape(-1)
    onehot = (route_ids[:, None] == jnp.arange(EXP, dtype=jnp.int32)[None, :]).astype(jnp.int32)
    before_count = jnp.cumsum(onehot, axis=0) - onehot
    slot_index = jnp.sum(before_count * onehot, axis=1)
    slot_range = jnp.arange(MOST, dtype=jnp.int32)
    placed = (onehot.T[:, None, :] == 1) & (slot_index[None, None, :] == slot_range[None, :, None])
    chooser = (
        jnp.sum(placed.reshape(EXP, MOST, tok_rows, 2).astype(jnp.float32), axis=3)
        .astype(jnp.bfloat16)
        .reshape(EXP * MOST, tok_rows)
    )
    weighted = jnp.sum(
        (placed.astype(jnp.float32) * route_gates.reshape(-1)[None, None, :]).reshape(
            EXP, MOST, tok_rows, 2
        ),
        axis=3,
    )
    group = ctx_count // EXP
    packed = (
        jnp.dot(chooser, normed_share, preferred_element_type=jnp.float32)
        .astype(jnp.bfloat16)
        .reshape(EXP, MOST, share_width)
    )
    by_group = lax.all_to_all(packed, "g", split_axis=0, concat_axis=0, tiled=True)
    arrived = lax.all_gather(by_group, ("j", "head"), axis=1, tiled=False)
    sources = ctx_count
    slots_now = arrived.shape[2]
    flat_rows = (
        arrived.reshape(EXP, group, head_count, slots_now, share_width)
        .transpose(0, 1, 3, 2, 4)
        .reshape(sources * slots_now, model_width)
    )
    gate_part = jnp.einsum("rd,fd->rf", flat_rows, expert_gate, preferred_element_type=jnp.float32)
    up_part = jnp.einsum("rd,fd->rf", flat_rows, expert_up, preferred_element_type=jnp.float32)
    hidden_units = (
        (jax.nn.silu(gate_part) * up_part).astype(jnp.bfloat16).reshape(sources, slots_now, -1)
    )
    joined = lax.all_gather(hidden_units, "head", axis=2, tiled=True)
    partial_value = jnp.einsum(
        "nmf,fd->nmd", joined, expert_down, preferred_element_type=jnp.float32
    ).astype(jnp.bfloat16)
    returned = lax.all_to_all(partial_value, ("g", "j"), split_axis=0, concat_axis=0, tiled=True)
    summed = jnp.sum(returned.astype(jnp.float32).reshape(EXP, group, MOST, share_width), axis=1)
    mixture = jnp.einsum("est,esd->td", weighted, summed, precision=highest)
    return (hidden_share + mixture).astype(jnp.bfloat16)


def solution(mesh):
    ctx_count = mesh.shape["ctx"]
    head_count = mesh.shape["head"]
    split = Mesh(
        mesh.devices.reshape(EXP, ctx_count // EXP, head_count), ("g", "j", "head")
    )
    ctx = ("g", "j")
    return jax.shard_map(
        body,
        mesh=split,
        in_specs=(
            P(ctx, "head"),
            P(ctx, "head"),
            P(ctx, "head"),
            P(ctx, "head"),
            P(ctx, "head"),
            P("head"),
            P("head", ctx, None),
            P(ctx, None),
            P(),
            P(),
            P(ctx, None),
            P(("g", "j", "head"), None),
            P(("g", "j", "head"), None),
            P(ctx, "head"),
        ),
        out_specs=P(ctx, "head"),
        check_vma=False,
    )
```

```python
import jax
import jax.numpy as jnp
from jax import lax
from jax.sharding import Mesh, PartitionSpec as P

EXP = 8
MOST = 10
CTX = ("g", "q", "core")


epsilon = 1e-06
highest = lax.Precision.HIGHEST


def pack_state(factor, state):
    heads, dim, _ = state.shape
    extra = jnp.broadcast_to(factor[:, None, None], (heads, 8, dim))
    return jnp.concatenate([state, extra], axis=1)


def unpack_state(packed):
    dim = packed.shape[-1]
    return packed[:, dim, 0], packed[:, :dim, :]


def prefix_scan(factor, state, axis, count):
    place = lax.axis_index(axis)

    def shift(value, distance):
        return lax.ppermute(value, axis, [(i, i + distance) for i in range(count - distance)])

    identity = pack_state(jnp.ones_like(factor), jnp.zeros_like(state))
    current = jnp.where(place >= 1, shift(pack_state(factor, state), 1), identity)
    distance = 1
    while distance < count:
        earlier_factor, earlier_state = unpack_state(shift(current, distance))
        later_factor, later_state = unpack_state(current)
        joined = pack_state(
            earlier_factor * later_factor,
            later_factor[:, None, None] * earlier_state + later_state,
        )
        current = jnp.where(place >= distance, joined, current)
        distance *= 2
    return unpack_state(current)[1]


def body(
    queries,
    key_heads,
    value_heads,
    gate_logits,
    log_decay,
    attn_gain,
    out_weight,
    residual,
    norm_gain,
    router_weight,
    expert_ids,
    expert_gate,
    expert_up,
    expert_down,
):
    ctx_count = lax.axis_size(CTX)
    head_count = lax.axis_size("head")
    head_index = lax.axis_index("head")
    tok_rows = queries.shape[0]
    local_heads = log_decay.shape[1]
    head_dim = queries.shape[1] // local_heads
    model_width = residual.shape[1]
    share_width = model_width // head_count
    query_blocks = queries.reshape(tok_rows, local_heads, head_dim)
    key_blocks = key_heads.reshape(tok_rows, local_heads, head_dim)
    value_blocks = value_heads.reshape(tok_rows, local_heads, head_dim)
    cumulative = jnp.cumsum(log_decay, axis=0)
    block_total = cumulative[-1]
    keys_decayed = (
        key_blocks.astype(jnp.float32) * jnp.exp(block_total[None, :] - cumulative)[:, :, None]
    ).astype(jnp.bfloat16)
    local_state = jnp.einsum(
        "thd,the->hde", keys_decayed, value_blocks, preferred_element_type=jnp.float32
    )
    entering = prefix_scan(jnp.exp(block_total), local_state, CTX, ctx_count)
    sequence_offsets = jnp.arange(tok_rows)
    causal = (sequence_offsets[:, None] >= sequence_offsets[None, :])[None, :, :]
    cum_heads = cumulative.T
    decay_gaps = jnp.where(causal, cum_heads[:, :, None] - cum_heads[:, None, :], 0.0)
    scores = jnp.einsum(
        "thd,shd->hts", query_blocks, key_blocks, preferred_element_type=jnp.float32
    )
    attn_probs = jnp.where(causal, scores * jnp.exp(decay_gaps), 0.0).astype(jnp.bfloat16)
    within = jnp.einsum(
        "hts,shd->thd", attn_probs, value_blocks, preferred_element_type=jnp.float32
    )
    carried = jnp.einsum(
        "thd,hde->the", query_blocks.astype(jnp.float32), entering, precision=highest
    )
    attended = within + carried * jnp.exp(cumulative)[:, :, None]
    rms_scale = lax.rsqrt(jnp.mean(attended * attended, axis=-1, keepdims=True) + epsilon)
    gate_open = jax.nn.sigmoid(
        gate_logits.astype(jnp.float32).reshape(tok_rows, local_heads, head_dim)
    )
    attn_mixed = (
        attended * rms_scale * attn_gain.reshape(local_heads, head_dim) * gate_open
    ).astype(jnp.bfloat16)
    core = lax.axis_index("core")
    swap = [(0, 1), (1, 0)]
    half_width = share_width // 2
    split_weight = out_weight.reshape(local_heads, -1, head_count, 2, half_width)
    mine = jnp.where(core == 0, split_weight[:, :, :, 0], split_weight[:, :, :, 1])
    theirs = jnp.where(core == 0, split_weight[:, :, :, 1], split_weight[:, :, :, 0])
    received = lax.ppermute(theirs, "core", swap)
    pair_rows = jnp.concatenate(
        [jnp.where(core == 0, mine, received), jnp.where(core == 0, received, mine)], axis=1
    )
    row_whole = lax.all_gather(pair_rows, ("g", "q"), axis=1, tiled=True)
    partner_mixed = lax.ppermute(attn_mixed, "core", swap)
    both_mixed = jnp.concatenate(
        [jnp.where(core == 0, attn_mixed, partner_mixed), jnp.where(core == 0, partner_mixed, attn_mixed)],
        axis=0,
    )
    partial_sum = jnp.einsum(
        "thr,hrqd->tqd", both_mixed, row_whole, preferred_element_type=jnp.float32
    )
    scattered = lax.psum_scatter(
        partial_sum.astype(jnp.bfloat16), "head", scatter_dimension=1, tiled=True
    ).reshape(2, tok_rows, half_width)
    own_rows = jnp.where(core == 0, scattered[0], scattered[1])
    other_rows = lax.ppermute(jnp.where(core == 0, scattered[1], scattered[0]), "core", swap)
    projected = jnp.concatenate(
        [jnp.where(core == 0, own_rows, other_rows), jnp.where(core == 0, other_rows, own_rows)],
        axis=1,
    ).astype(jnp.float32)
    share_start = head_index * share_width
    residual_share = lax.dynamic_slice_in_dim(residual, share_start, share_width, 1)
    gain_share = lax.dynamic_slice_in_dim(norm_gain, share_start, share_width, 0)
    router_share = lax.dynamic_slice_in_dim(router_weight, share_start, share_width, 0)
    hidden_share = residual_share.astype(jnp.float32) + projected
    router_part = jnp.dot(
        hidden_share * gain_share[None, :],
        router_share.astype(jnp.float32),
        precision=highest,
    )
    square_part = jnp.sum(hidden_share * hidden_share, axis=-1, keepdims=True)
    stats = lax.psum(jnp.concatenate([square_part, router_part], axis=1), "head")
    row_scale = lax.rsqrt(stats[:, :1] / model_width + epsilon)
    logits = stats[:, 1:] * row_scale
    normed_share = (hidden_share * row_scale * gain_share[None, :]).astype(jnp.bfloat16)
    columns = jnp.arange(router_weight.shape[1], dtype=jnp.int32)
    picked = jnp.sum(
        jnp.where(columns[None, None, :] == expert_ids[:, :, None], logits[:, None, :], 0.0),
        axis=-1,
    )
    route_gates = jax.nn.sigmoid(picked - picked[:, ::-1])
    route_ids = expert_ids.reshape(-1)
    onehot = (route_ids[:, None] == jnp.arange(EXP, dtype=jnp.int32)[None, :]).astype(jnp.int32)
    before_count = jnp.cumsum(onehot, axis=0) - onehot
    slot_index = jnp.sum(before_count * onehot, axis=1)
    slot_range = jnp.arange(MOST, dtype=jnp.int32)
    placed = (onehot.T[:, None, :] == 1) & (slot_index[None, None, :] == slot_range[None, :, None])
    chooser = (
        jnp.sum(placed.reshape(EXP, MOST, tok_rows, 2).astype(jnp.float32), axis=3)
        .astype(jnp.bfloat16)
        .reshape(EXP * MOST, tok_rows)
    )
    weighted = jnp.sum(
        (placed.astype(jnp.float32) * route_gates.reshape(-1)[None, None, :]).reshape(
            EXP, MOST, tok_rows, 2
        ),
        axis=3,
    )
    group = ctx_count // EXP
    packed = (
        jnp.dot(chooser, normed_share, preferred_element_type=jnp.float32)
        .astype(jnp.bfloat16)
        .reshape(EXP, MOST, share_width)
    )
    by_group = lax.all_to_all(packed, "g", split_axis=0, concat_axis=0, tiled=True)
    arrived = lax.all_gather(by_group, ("q", "core", "head"), axis=1, tiled=False)
    sources = ctx_count
    slots_now = arrived.shape[2]
    flat_rows = (
        arrived.reshape(EXP, group, head_count, slots_now, share_width)
        .transpose(0, 1, 3, 2, 4)
        .reshape(sources * slots_now, model_width)
    )
    gate_part = jnp.einsum("rd,fd->rf", flat_rows, expert_gate, preferred_element_type=jnp.float32)
    up_part = jnp.einsum("rd,fd->rf", flat_rows, expert_up, preferred_element_type=jnp.float32)
    hidden_units = (
        (jax.nn.silu(gate_part) * up_part).astype(jnp.bfloat16).reshape(sources, slots_now, -1)
    )
    joined = lax.all_gather(hidden_units, "head", axis=2, tiled=True)
    partial_value = jnp.einsum(
        "nmf,fd->nmd", joined, expert_down, preferred_element_type=jnp.float32
    ).astype(jnp.bfloat16)
    returned = lax.all_to_all(partial_value, CTX, split_axis=0, concat_axis=0, tiled=True)
    summed = jnp.sum(returned.astype(jnp.float32).reshape(EXP, group, MOST, share_width), axis=1)
    mixture = jnp.einsum("est,esd->td", weighted, summed, precision=highest)
    return (hidden_share + mixture).astype(jnp.bfloat16)


def solution(mesh):
    ctx_count = mesh.shape["ctx"]
    head_count = mesh.shape["head"]
    split = Mesh(
        mesh.devices.reshape(EXP, ctx_count // EXP // 2, 2, head_count), ("g", "q", "core", "head")
    )
    ctx = CTX
    return jax.shard_map(
        body,
        mesh=split,
        in_specs=(
            P(ctx, "head"),
            P(ctx, "head"),
            P(ctx, "head"),
            P(ctx, "head"),
            P(ctx, "head"),
            P("head"),
            P("head", ctx, None),
            P(ctx, None),
            P(),
            P(),
            P(ctx, None),
            P(ctx + ("head",), None),
            P(ctx + ("head",), None),
            P(ctx, "head"),
        ),
        out_specs=P(ctx, "head"),
        check_vma=False,
    )
```

```python
import jax
import jax.numpy as jnp
from jax import lax
from jax.sharding import Mesh, PartitionSpec as P

EXP = 8
MOST = 10
CTX = ("g", "q", "core")


epsilon = 1e-06
highest = lax.Precision.HIGHEST


def pack_state(factor, state):
    heads, dim, _ = state.shape
    extra = jnp.broadcast_to(factor[:, None, None], (heads, 8, dim))
    return jnp.concatenate([state, extra], axis=1)


def unpack_state(packed):
    dim = packed.shape[-1]
    return packed[:, dim, 0], packed[:, :dim, :]


def prefix_scan(factor, state, axis, count):
    place = lax.axis_index(axis)

    def shift(value, distance):
        return lax.ppermute(value, axis, [(i, i + distance) for i in range(count - distance)])

    identity = pack_state(jnp.ones_like(factor), jnp.zeros_like(state))
    current = jnp.where(place >= 1, shift(pack_state(factor, state), 1), identity)
    distance = 1
    while distance < count:
        earlier_factor, earlier_state = unpack_state(shift(current, distance))
        later_factor, later_state = unpack_state(current)
        joined = pack_state(
            earlier_factor * later_factor,
            later_factor[:, None, None] * earlier_state + later_state,
        )
        current = jnp.where(place >= distance, joined, current)
        distance *= 2
    return unpack_state(current)[1]


def body(
    queries,
    key_heads,
    value_heads,
    gate_logits,
    log_decay,
    attn_gain,
    out_weight,
    residual,
    norm_gain,
    router_weight,
    expert_ids,
    expert_gate,
    expert_up,
    expert_down,
):
    ctx_count = lax.axis_size(CTX)
    head_count = lax.axis_size("head")
    head_index = lax.axis_index("head")
    tok_rows = queries.shape[0]
    local_heads = log_decay.shape[1]
    head_dim = queries.shape[1] // local_heads
    model_width = residual.shape[1]
    share_width = model_width // head_count
    query_blocks = queries.reshape(tok_rows, local_heads, head_dim)
    key_blocks = key_heads.reshape(tok_rows, local_heads, head_dim)
    value_blocks = value_heads.reshape(tok_rows, local_heads, head_dim)
    cumulative = jnp.cumsum(log_decay, axis=0)
    block_total = cumulative[-1]
    keys_decayed = (
        key_blocks.astype(jnp.float32) * jnp.exp(block_total[None, :] - cumulative)[:, :, None]
    ).astype(jnp.bfloat16)
    local_state = jnp.einsum(
        "thd,the->hde", keys_decayed, value_blocks, preferred_element_type=jnp.float32
    )
    core = lax.axis_index("core")
    swap = [(0, 1), (1, 0)]
    factor = jnp.exp(block_total)
    partner_factor, partner_state = unpack_state(
        lax.ppermute(pack_state(factor, local_state), "core", swap)
    )
    first_factor = jnp.where(core == 0, factor, partner_factor)
    first_state = jnp.where(core == 0, local_state, partner_state)
    second_factor = jnp.where(core == 0, partner_factor, factor)
    second_state = jnp.where(core == 0, partner_state, local_state)
    chip_factor = first_factor * second_factor
    chip_state = second_factor[:, None, None] * first_state + second_state
    half = local_heads // 2
    half_factor = jnp.where(core == 0, chip_factor[:half], chip_factor[half:])
    half_state = jnp.where(core == 0, chip_state[:half], chip_state[half:])
    mine = prefix_scan(half_factor, half_state, ("g", "q"), ctx_count // 2)
    other = lax.ppermute(mine, "core", swap)
    chip_entering = jnp.concatenate(
        [jnp.where(core == 0, mine, other), jnp.where(core == 0, other, mine)], axis=0
    )
    entering = jnp.where(
        core == 0, chip_entering, first_factor[:, None, None] * chip_entering + first_state
    )
    sequence_offsets = jnp.arange(tok_rows)
    causal = (sequence_offsets[:, None] >= sequence_offsets[None, :])[None, :, :]
    cum_heads = cumulative.T
    decay_gaps = jnp.where(causal, cum_heads[:, :, None] - cum_heads[:, None, :], 0.0)
    scores = jnp.einsum(
        "thd,shd->hts", query_blocks, key_blocks, preferred_element_type=jnp.float32
    )
    attn_probs = jnp.where(causal, scores * jnp.exp(decay_gaps), 0.0).astype(jnp.bfloat16)
    within = jnp.einsum(
        "hts,shd->thd", attn_probs, value_blocks, preferred_element_type=jnp.float32
    )
    carried = jnp.einsum(
        "thd,hde->the", query_blocks.astype(jnp.float32), entering, precision=highest
    )
    attended = within + carried * jnp.exp(cumulative)[:, :, None]
    rms_scale = lax.rsqrt(jnp.mean(attended * attended, axis=-1, keepdims=True) + epsilon)
    gate_open = jax.nn.sigmoid(
        gate_logits.astype(jnp.float32).reshape(tok_rows, local_heads, head_dim)
    )
    attn_mixed = (
        attended * rms_scale * attn_gain.reshape(local_heads, head_dim) * gate_open
    ).astype(jnp.bfloat16)
    half_width = share_width // 2
    split_weight = out_weight.reshape(local_heads, -1, head_count, 2, half_width)
    mine = jnp.where(core == 0, split_weight[:, :, :, 0], split_weight[:, :, :, 1])
    theirs = jnp.where(core == 0, split_weight[:, :, :, 1], split_weight[:, :, :, 0])
    received = lax.ppermute(theirs, "core", swap)
    pair_rows = jnp.concatenate(
        [jnp.where(core == 0, mine, received), jnp.where(core == 0, received, mine)], axis=1
    )
    row_whole = lax.all_gather(pair_rows, ("g", "q"), axis=1, tiled=True)
    partner_mixed = lax.ppermute(attn_mixed, "core", swap)
    both_mixed = jnp.concatenate(
        [jnp.where(core == 0, attn_mixed, partner_mixed), jnp.where(core == 0, partner_mixed, attn_mixed)],
        axis=0,
    )
    partial_sum = jnp.einsum(
        "thr,hrqd->tqd", both_mixed, row_whole, preferred_element_type=jnp.float32
    )
    scattered = lax.psum_scatter(
        partial_sum.astype(jnp.bfloat16), "head", scatter_dimension=1, tiled=True
    ).reshape(2, tok_rows, half_width)
    own_rows = jnp.where(core == 0, scattered[0], scattered[1])
    other_rows = lax.ppermute(jnp.where(core == 0, scattered[1], scattered[0]), "core", swap)
    projected = jnp.concatenate(
        [jnp.where(core == 0, own_rows, other_rows), jnp.where(core == 0, other_rows, own_rows)],
        axis=1,
    ).astype(jnp.float32)
    share_start = head_index * share_width
    residual_share = lax.dynamic_slice_in_dim(residual, share_start, share_width, 1)
    gain_share = lax.dynamic_slice_in_dim(norm_gain, share_start, share_width, 0)
    router_share = lax.dynamic_slice_in_dim(router_weight, share_start, share_width, 0)
    hidden_share = residual_share.astype(jnp.float32) + projected
    router_part = jnp.dot(
        hidden_share * gain_share[None, :],
        router_share.astype(jnp.float32),
        precision=highest,
    )
    square_part = jnp.sum(hidden_share * hidden_share, axis=-1, keepdims=True)
    stats = lax.psum(jnp.concatenate([square_part, router_part], axis=1), "head")
    row_scale = lax.rsqrt(stats[:, :1] / model_width + epsilon)
    logits = stats[:, 1:] * row_scale
    normed_share = (hidden_share * row_scale * gain_share[None, :]).astype(jnp.bfloat16)
    columns = jnp.arange(router_weight.shape[1], dtype=jnp.int32)
    picked = jnp.sum(
        jnp.where(columns[None, None, :] == expert_ids[:, :, None], logits[:, None, :], 0.0),
        axis=-1,
    )
    route_gates = jax.nn.sigmoid(picked - picked[:, ::-1])
    route_ids = expert_ids.reshape(-1)
    onehot = (route_ids[:, None] == jnp.arange(EXP, dtype=jnp.int32)[None, :]).astype(jnp.int32)
    before_count = jnp.cumsum(onehot, axis=0) - onehot
    slot_index = jnp.sum(before_count * onehot, axis=1)
    slot_range = jnp.arange(MOST, dtype=jnp.int32)
    placed = (onehot.T[:, None, :] == 1) & (slot_index[None, None, :] == slot_range[None, :, None])
    chooser = (
        jnp.sum(placed.reshape(EXP, MOST, tok_rows, 2).astype(jnp.float32), axis=3)
        .astype(jnp.bfloat16)
        .reshape(EXP * MOST, tok_rows)
    )
    weighted = jnp.sum(
        (placed.astype(jnp.float32) * route_gates.reshape(-1)[None, None, :]).reshape(
            EXP, MOST, tok_rows, 2
        ),
        axis=3,
    )
    group = ctx_count // EXP
    packed = (
        jnp.dot(chooser, normed_share, preferred_element_type=jnp.float32)
        .astype(jnp.bfloat16)
        .reshape(EXP, MOST, share_width)
    )
    by_group = lax.all_to_all(packed, "g", split_axis=0, concat_axis=0, tiled=True)
    arrived = lax.all_gather(by_group, ("q", "core", "head"), axis=1, tiled=False)
    sources = ctx_count
    slots_now = arrived.shape[2]
    flat_rows = (
        arrived.reshape(EXP, group, head_count, slots_now, share_width)
        .transpose(0, 1, 3, 2, 4)
        .reshape(sources * slots_now, model_width)
    )
    gate_part = jnp.einsum("rd,fd->rf", flat_rows, expert_gate, preferred_element_type=jnp.float32)
    up_part = jnp.einsum("rd,fd->rf", flat_rows, expert_up, preferred_element_type=jnp.float32)
    hidden_units = (
        (jax.nn.silu(gate_part) * up_part).astype(jnp.bfloat16).reshape(sources, slots_now, -1)
    )
    joined = lax.all_gather(hidden_units, "head", axis=2, tiled=True)
    partial_value = jnp.einsum(
        "nmf,fd->nmd", joined, expert_down, preferred_element_type=jnp.float32
    ).astype(jnp.bfloat16)
    returned = lax.all_to_all(partial_value, CTX, split_axis=0, concat_axis=0, tiled=True)
    summed = jnp.sum(returned.astype(jnp.float32).reshape(EXP, group, MOST, share_width), axis=1)
    mixture = jnp.einsum("est,esd->td", weighted, summed, precision=highest)
    return (hidden_share + mixture).astype(jnp.bfloat16)


def solution(mesh):
    ctx_count = mesh.shape["ctx"]
    head_count = mesh.shape["head"]
    split = Mesh(
        mesh.devices.reshape(EXP, ctx_count // EXP // 2, 2, head_count), ("g", "q", "core", "head")
    )
    ctx = CTX
    return jax.shard_map(
        body,
        mesh=split,
        in_specs=(
            P(ctx, "head"),
            P(ctx, "head"),
            P(ctx, "head"),
            P(ctx, "head"),
            P(ctx, "head"),
            P("head"),
            P("head", ctx, None),
            P(ctx, None),
            P(),
            P(),
            P(ctx, None),
            P(ctx + ("head",), None),
            P(ctx + ("head",), None),
            P(ctx, "head"),
        ),
        out_specs=P(ctx, "head"),
        check_vma=False,
    )
```

```python
import jax
import jax.numpy as jnp
from jax import lax
from jax.sharding import Mesh, PartitionSpec as P

EXP = 8
MOST = 10
CTX = ("g", "q", "core")


epsilon = 1e-06
highest = lax.Precision.HIGHEST


def pack_state(factor, state):
    heads, dim, _ = state.shape
    extra = jnp.broadcast_to(factor[:, None, None], (heads, 8, dim))
    return jnp.concatenate([state, extra], axis=1)


def unpack_state(packed):
    dim = packed.shape[-1]
    return packed[:, dim, 0], packed[:, :dim, :]


def prefix_scan(factor, state, axis, count):
    place = lax.axis_index(axis)

    def shift(value, distance):
        return lax.ppermute(value, axis, [(i, i + distance) for i in range(count - distance)])

    identity = pack_state(jnp.ones_like(factor), jnp.zeros_like(state))
    current = jnp.where(place >= 1, shift(pack_state(factor, state), 1), identity)
    distance = 1
    while distance < count:
        earlier_factor, earlier_state = unpack_state(shift(current, distance))
        later_factor, later_state = unpack_state(current)
        joined = pack_state(
            earlier_factor * later_factor,
            later_factor[:, None, None] * earlier_state + later_state,
        )
        current = jnp.where(place >= distance, joined, current)
        distance *= 2
    return unpack_state(current)[1]


def body(
    queries,
    key_heads,
    value_heads,
    gate_logits,
    log_decay,
    attn_gain,
    out_weight,
    residual,
    norm_gain,
    router_weight,
    expert_ids,
    expert_gate,
    expert_up,
    expert_down,
):
    ctx_count = lax.axis_size(CTX)
    head_count = lax.axis_size("head")
    head_index = lax.axis_index("head")
    tok_rows = queries.shape[0]
    local_heads = log_decay.shape[1]
    head_dim = queries.shape[1] // local_heads
    model_width = residual.shape[1]
    share_width = model_width // head_count
    query_blocks = queries.reshape(tok_rows, local_heads, head_dim)
    key_blocks = key_heads.reshape(tok_rows, local_heads, head_dim)
    value_blocks = value_heads.reshape(tok_rows, local_heads, head_dim)
    cumulative = jnp.cumsum(log_decay, axis=0)
    block_total = cumulative[-1]
    keys_decayed = (
        key_blocks.astype(jnp.float32) * jnp.exp(block_total[None, :] - cumulative)[:, :, None]
    ).astype(jnp.bfloat16)
    local_state = jnp.einsum(
        "thd,the->hde", keys_decayed, value_blocks, preferred_element_type=jnp.float32
    )
    core = lax.axis_index("core")
    swap = [(0, 1), (1, 0)]
    factor = jnp.exp(block_total)
    partner_factor, partner_state = unpack_state(
        lax.ppermute(pack_state(factor, local_state), "core", swap)
    )
    first_factor = jnp.where(core == 0, factor, partner_factor)
    first_state = jnp.where(core == 0, local_state, partner_state)
    second_factor = jnp.where(core == 0, partner_factor, factor)
    second_state = jnp.where(core == 0, partner_state, local_state)
    chip_factor = first_factor * second_factor
    chip_state = second_factor[:, None, None] * first_state + second_state
    half = local_heads // 2
    half_factor = jnp.where(core == 0, chip_factor[:half], chip_factor[half:])
    half_state = jnp.where(core == 0, chip_state[:half], chip_state[half:])
    mine = prefix_scan(half_factor, half_state, ("g", "q"), ctx_count // 2)
    other = lax.ppermute(mine, "core", swap)
    chip_entering = jnp.concatenate(
        [jnp.where(core == 0, mine, other), jnp.where(core == 0, other, mine)], axis=0
    )
    entering = jnp.where(
        core == 0, chip_entering, first_factor[:, None, None] * chip_entering + first_state
    )
    sequence_offsets = jnp.arange(tok_rows)
    causal = (sequence_offsets[:, None] >= sequence_offsets[None, :])[None, :, :]
    cum_heads = cumulative.T
    decay_gaps = jnp.where(causal, cum_heads[:, :, None] - cum_heads[:, None, :], 0.0)
    scores = jnp.einsum(
        "thd,shd->hts", query_blocks, key_blocks, preferred_element_type=jnp.float32
    )
    attn_probs = jnp.where(causal, scores * jnp.exp(decay_gaps), 0.0).astype(jnp.bfloat16)
    within = jnp.einsum(
        "hts,shd->thd", attn_probs, value_blocks, preferred_element_type=jnp.float32
    )
    carried = jnp.einsum(
        "thd,hde->the", query_blocks.astype(jnp.float32), entering, precision=highest
    )
    attended = within + carried * jnp.exp(cumulative)[:, :, None]
    rms_scale = lax.rsqrt(jnp.mean(attended * attended, axis=-1, keepdims=True) + epsilon)
    gate_open = jax.nn.sigmoid(
        gate_logits.astype(jnp.float32).reshape(tok_rows, local_heads, head_dim)
    )
    attn_mixed = (
        attended * rms_scale * attn_gain.reshape(local_heads, head_dim) * gate_open
    ).astype(jnp.bfloat16)
    half_width = share_width // 2
    split_weight = out_weight.reshape(local_heads, -1, head_count, 2, half_width)
    mine = jnp.where(core == 0, split_weight[:, :, :, 0], split_weight[:, :, :, 1])
    theirs = jnp.where(core == 0, split_weight[:, :, :, 1], split_weight[:, :, :, 0])
    received = lax.ppermute(theirs, "core", swap)
    pair_rows = jnp.concatenate(
        [jnp.where(core == 0, mine, received), jnp.where(core == 0, received, mine)], axis=1
    )
    row_whole = lax.all_gather(pair_rows, ("g", "q"), axis=1, tiled=True)
    partner_mixed = lax.ppermute(attn_mixed, "core", swap)
    both_mixed = jnp.concatenate(
        [jnp.where(core == 0, attn_mixed, partner_mixed), jnp.where(core == 0, partner_mixed, attn_mixed)],
        axis=0,
    )
    partial_sum = jnp.einsum(
        "thr,hrqd->tqd", both_mixed, row_whole, preferred_element_type=jnp.float32
    )
    scattered = lax.psum_scatter(
        partial_sum.astype(jnp.bfloat16), "head", scatter_dimension=1, tiled=True
    ).reshape(2, tok_rows, half_width)
    own_rows = jnp.where(core == 0, scattered[0], scattered[1])
    other_rows = lax.ppermute(jnp.where(core == 0, scattered[1], scattered[0]), "core", swap)
    projected = jnp.concatenate(
        [jnp.where(core == 0, own_rows, other_rows), jnp.where(core == 0, other_rows, own_rows)],
        axis=1,
    ).astype(jnp.float32)
    share_start = head_index * share_width
    residual_share = lax.dynamic_slice_in_dim(residual, share_start, share_width, 1)
    gain_share = lax.dynamic_slice_in_dim(norm_gain, share_start, share_width, 0)
    router_share = lax.dynamic_slice_in_dim(router_weight, share_start, share_width, 0)
    hidden_share = residual_share.astype(jnp.float32) + projected
    router_part = jnp.dot(
        hidden_share * gain_share[None, :],
        router_share.astype(jnp.float32),
        precision=highest,
    )
    square_part = jnp.sum(hidden_share * hidden_share, axis=-1, keepdims=True)
    stats = lax.psum(jnp.concatenate([square_part, router_part], axis=1), "head")
    row_scale = lax.rsqrt(stats[:, :1] / model_width + epsilon)
    logits = stats[:, 1:] * row_scale
    normed_share = (hidden_share * row_scale * gain_share[None, :]).astype(jnp.bfloat16)
    columns = jnp.arange(router_weight.shape[1], dtype=jnp.int32)
    picked = jnp.sum(
        jnp.where(columns[None, None, :] == expert_ids[:, :, None], logits[:, None, :], 0.0),
        axis=-1,
    )
    route_gates = jax.nn.sigmoid(picked - picked[:, ::-1])
    route_ids = expert_ids.reshape(-1)
    onehot = (route_ids[:, None] == jnp.arange(EXP, dtype=jnp.int32)[None, :]).astype(jnp.int32)
    before_count = jnp.cumsum(onehot, axis=0) - onehot
    slot_index = jnp.sum(before_count * onehot, axis=1)
    slot_range = jnp.arange(MOST, dtype=jnp.int32)
    placed = (onehot.T[:, None, :] == 1) & (slot_index[None, None, :] == slot_range[None, :, None])
    chooser = (
        jnp.sum(placed.reshape(EXP, MOST, tok_rows, 2).astype(jnp.float32), axis=3)
        .astype(jnp.bfloat16)
        .reshape(EXP * MOST, tok_rows)
    )
    weighted = jnp.sum(
        (placed.astype(jnp.float32) * route_gates.reshape(-1)[None, None, :]).reshape(
            EXP, MOST, tok_rows, 2
        ),
        axis=3,
    )
    group = ctx_count // EXP
    packed = (
        jnp.dot(chooser, normed_share, preferred_element_type=jnp.float32)
        .astype(jnp.bfloat16)
        .reshape(EXP, MOST, share_width)
    )
    by_group = lax.all_to_all(packed, "g", split_axis=0, concat_axis=0, tiled=True)
    own_parity = lax.all_gather(by_group, ("q", "head"), axis=1, tiled=False)
    other_parity = lax.ppermute(own_parity, "core", swap)
    pairs = group // 2
    arrived = jnp.stack(
        [
            jnp.where(core == 0, own_parity, other_parity),
            jnp.where(core == 0, other_parity, own_parity),
        ],
        axis=2,
    ).reshape(EXP, pairs, head_count, 2, MOST, share_width)
    sources = ctx_count
    slots_now = MOST
    flat_rows = arrived.transpose(0, 1, 3, 4, 2, 5).reshape(sources * slots_now, model_width)
    gate_part = jnp.einsum("rd,fd->rf", flat_rows, expert_gate, preferred_element_type=jnp.float32)
    up_part = jnp.einsum("rd,fd->rf", flat_rows, expert_up, preferred_element_type=jnp.float32)
    hidden_units = (
        (jax.nn.silu(gate_part) * up_part).astype(jnp.bfloat16).reshape(sources, slots_now, -1)
    )
    joined = lax.all_gather(hidden_units, "head", axis=2, tiled=True)
    partial_value = jnp.einsum(
        "nmf,fd->nmd", joined, expert_down, preferred_element_type=jnp.float32
    ).astype(jnp.bfloat16)
    by_parity = partial_value.reshape(EXP * pairs, 2, slots_now, share_width)
    keep = jnp.where(core == 0, by_parity[:, 0], by_parity[:, 1])
    give = jnp.where(core == 0, by_parity[:, 1], by_parity[:, 0])
    pair_sum = (
        keep.astype(jnp.float32) + lax.ppermute(give, "core", swap).astype(jnp.float32)
    ).astype(jnp.bfloat16)
    returned = lax.all_to_all(pair_sum, ("g", "q"), split_axis=0, concat_axis=0, tiled=True)
    summed = jnp.sum(returned.astype(jnp.float32).reshape(EXP, pairs, MOST, share_width), axis=1)
    mixture = jnp.einsum("est,esd->td", weighted, summed, precision=highest)
    return (hidden_share + mixture).astype(jnp.bfloat16)


def solution(mesh):
    ctx_count = mesh.shape["ctx"]
    head_count = mesh.shape["head"]
    split = Mesh(
        mesh.devices.reshape(EXP, ctx_count // EXP // 2, 2, head_count), ("g", "q", "core", "head")
    )
    ctx = CTX
    return jax.shard_map(
        body,
        mesh=split,
        in_specs=(
            P(ctx, "head"),
            P(ctx, "head"),
            P(ctx, "head"),
            P(ctx, "head"),
            P(ctx, "head"),
            P("head"),
            P("head", ctx, None),
            P(ctx, None),
            P(),
            P(),
            P(ctx, None),
            P(ctx + ("head",), None),
            P(ctx + ("head",), None),
            P(ctx, "head"),
        ),
        out_specs=P(ctx, "head"),
        check_vma=False,
    )
```

```python
import jax
import jax.numpy as jnp
from jax import lax
from jax.sharding import Mesh, PartitionSpec as P

EXP = 8
MOST = 10
CTX = ("g", "q", "core")


epsilon = 1e-06
highest = lax.Precision.HIGHEST


def pack_state(factor, state):
    heads, dim, _ = state.shape
    extra = jnp.broadcast_to(factor[:, None, None], (heads, 8, dim))
    return jnp.concatenate([state, extra], axis=1)


def unpack_state(packed):
    dim = packed.shape[-1]
    return packed[:, dim, 0], packed[:, :dim, :]


def prefix_scan(factor, state, axis, count):
    place = lax.axis_index(axis)

    def shift(value, distance):
        return lax.ppermute(value, axis, [(i, i + distance) for i in range(count - distance)])

    identity = pack_state(jnp.ones_like(factor), jnp.zeros_like(state))
    current = jnp.where(place >= 1, shift(pack_state(factor, state), 1), identity)
    distance = 1
    while distance < count:
        earlier_factor, earlier_state = unpack_state(shift(current, distance))
        later_factor, later_state = unpack_state(current)
        joined = pack_state(
            earlier_factor * later_factor,
            later_factor[:, None, None] * earlier_state + later_state,
        )
        current = jnp.where(place >= distance, joined, current)
        distance *= 2
    return unpack_state(current)[1]


def body(
    queries,
    key_heads,
    value_heads,
    gate_logits,
    log_decay,
    attn_gain,
    out_weight,
    residual,
    norm_gain,
    router_weight,
    expert_ids,
    expert_gate,
    expert_up,
    expert_down,
):
    ctx_count = lax.axis_size(CTX)
    head_count = lax.axis_size("head")
    head_index = lax.axis_index("head")
    tok_rows = queries.shape[0]
    local_heads = log_decay.shape[1]
    head_dim = queries.shape[1] // local_heads
    model_width = residual.shape[1]
    share_width = model_width // head_count
    query_blocks = queries.reshape(tok_rows, local_heads, head_dim)
    key_blocks = key_heads.reshape(tok_rows, local_heads, head_dim)
    value_blocks = value_heads.reshape(tok_rows, local_heads, head_dim)
    cumulative = jnp.cumsum(log_decay, axis=0)
    block_total = cumulative[-1]
    keys_decayed = (
        key_blocks.astype(jnp.float32) * jnp.exp(block_total[None, :] - cumulative)[:, :, None]
    ).astype(jnp.bfloat16)
    local_state = jnp.einsum(
        "thd,the->hde", keys_decayed, value_blocks, preferred_element_type=jnp.float32
    )
    core = lax.axis_index("core")
    swap = [(0, 1), (1, 0)]
    factor = jnp.exp(block_total)
    partner_factor, partner_state = unpack_state(
        lax.ppermute(pack_state(factor, local_state), "core", swap)
    )
    first_factor = jnp.where(core == 0, factor, partner_factor)
    first_state = jnp.where(core == 0, local_state, partner_state)
    second_factor = jnp.where(core == 0, partner_factor, factor)
    second_state = jnp.where(core == 0, partner_state, local_state)
    chip_factor = first_factor * second_factor
    chip_state = second_factor[:, None, None] * first_state + second_state
    half = local_heads // 2
    half_factor = jnp.where(core == 0, chip_factor[:half], chip_factor[half:])
    half_state = jnp.where(core == 0, chip_state[:half], chip_state[half:])
    mine = prefix_scan(half_factor, half_state, ("g", "q"), ctx_count // 2)
    other = lax.ppermute(mine, "core", swap)
    chip_entering = jnp.concatenate(
        [jnp.where(core == 0, mine, other), jnp.where(core == 0, other, mine)], axis=0
    )
    entering = jnp.where(
        core == 0, chip_entering, first_factor[:, None, None] * chip_entering + first_state
    )
    sequence_offsets = jnp.arange(tok_rows)
    causal = (sequence_offsets[:, None] >= sequence_offsets[None, :])[None, :, :]
    cum_heads = cumulative.T
    decay_gaps = jnp.where(causal, cum_heads[:, :, None] - cum_heads[:, None, :], 0.0)
    scores = jnp.einsum(
        "thd,shd->hts", query_blocks, key_blocks, preferred_element_type=jnp.float32
    )
    attn_probs = jnp.where(causal, scores * jnp.exp(decay_gaps), 0.0).astype(jnp.bfloat16)
    within = jnp.einsum(
        "hts,shd->thd", attn_probs, value_blocks, preferred_element_type=jnp.float32
    )
    carried = jnp.einsum(
        "thd,hde->the", query_blocks.astype(jnp.float32), entering, precision=highest
    )
    attended = within + carried * jnp.exp(cumulative)[:, :, None]
    rms_scale = lax.rsqrt(jnp.mean(attended * attended, axis=-1, keepdims=True) + epsilon)
    gate_open = jax.nn.sigmoid(
        gate_logits.astype(jnp.float32).reshape(tok_rows, local_heads, head_dim)
    )
    attn_mixed = (
        attended * rms_scale * attn_gain.reshape(local_heads, head_dim) * gate_open
    ).astype(jnp.bfloat16)
    half_width = share_width // 2
    split_weight = out_weight.reshape(local_heads, -1, head_count, 2, half_width)
    mine = jnp.where(core == 0, split_weight[:, :, :, 0], split_weight[:, :, :, 1])
    theirs = jnp.where(core == 0, split_weight[:, :, :, 1], split_weight[:, :, :, 0])
    received = lax.ppermute(theirs, "core", swap)
    pair_rows = jnp.concatenate(
        [jnp.where(core == 0, mine, received), jnp.where(core == 0, received, mine)], axis=1
    )
    row_whole = lax.all_gather(pair_rows, ("g", "q"), axis=1, tiled=True)
    partner_mixed = lax.ppermute(attn_mixed, "core", swap)
    both_mixed = jnp.concatenate(
        [jnp.where(core == 0, attn_mixed, partner_mixed), jnp.where(core == 0, partner_mixed, attn_mixed)],
        axis=0,
    )
    partial_sum = jnp.einsum(
        "thr,hrqd->tqd", both_mixed, row_whole, preferred_element_type=jnp.float32
    )
    scattered = lax.psum_scatter(
        partial_sum.astype(jnp.bfloat16), "head", scatter_dimension=1, tiled=True
    ).reshape(2, tok_rows, half_width)
    own_rows = jnp.where(core == 0, scattered[0], scattered[1])
    other_rows = lax.ppermute(jnp.where(core == 0, scattered[1], scattered[0]), "core", swap)
    projected = jnp.concatenate(
        [jnp.where(core == 0, own_rows, other_rows), jnp.where(core == 0, other_rows, own_rows)],
        axis=1,
    ).astype(jnp.float32)
    share_start = head_index * share_width
    residual_share = lax.dynamic_slice_in_dim(residual, share_start, share_width, 1)
    gain_share = lax.dynamic_slice_in_dim(norm_gain, share_start, share_width, 0)
    router_share = lax.dynamic_slice_in_dim(router_weight, share_start, share_width, 0)
    hidden_share = residual_share.astype(jnp.float32) + projected
    router_part = jnp.dot(
        hidden_share * gain_share[None, :],
        router_share.astype(jnp.float32),
        precision=highest,
    )
    square_part = jnp.sum(hidden_share * hidden_share, axis=-1, keepdims=True)
    stats = lax.psum(jnp.concatenate([square_part, router_part], axis=1), "head")
    row_scale = lax.rsqrt(stats[:, :1] / model_width + epsilon)
    logits = stats[:, 1:] * row_scale
    normed_share = (hidden_share * row_scale * gain_share[None, :]).astype(jnp.bfloat16)
    columns = jnp.arange(router_weight.shape[1], dtype=jnp.int32)
    picked = jnp.sum(
        jnp.where(columns[None, None, :] == expert_ids[:, :, None], logits[:, None, :], 0.0),
        axis=-1,
    )
    route_gates = jax.nn.sigmoid(picked - picked[:, ::-1])
    route_ids = expert_ids.reshape(-1)
    onehot = (route_ids[:, None] == jnp.arange(EXP, dtype=jnp.int32)[None, :]).astype(jnp.int32)
    before_count = jnp.cumsum(onehot, axis=0) - onehot
    slot_index = jnp.sum(before_count * onehot, axis=1)
    slot_range = jnp.arange(MOST, dtype=jnp.int32)
    placed = (onehot.T[:, None, :] == 1) & (slot_index[None, None, :] == slot_range[None, :, None])
    chooser = (
        jnp.sum(placed.reshape(EXP, MOST, tok_rows, 2).astype(jnp.float32), axis=3)
        .astype(jnp.bfloat16)
        .reshape(EXP * MOST, tok_rows)
    )
    weighted = jnp.sum(
        (placed.astype(jnp.float32) * route_gates.reshape(-1)[None, None, :]).reshape(
            EXP, MOST, tok_rows, 2
        ),
        axis=3,
    )
    group = ctx_count // EXP
    packed = (
        jnp.dot(chooser, normed_share, preferred_element_type=jnp.float32)
        .astype(jnp.bfloat16)
        .reshape(EXP, MOST, share_width)
    )
    by_group = lax.all_to_all(packed, "g", split_axis=0, concat_axis=0, tiled=True)
    wide = lax.all_gather(by_group, "head", axis=2, tiled=True)
    own_parity = lax.all_gather(wide, "q", axis=0, tiled=False)
    other_parity = lax.ppermute(own_parity, "core", swap)
    pairs = group // 2
    halves = []
    for part in (own_parity, other_parity):
        part_rows = part.reshape(-1, model_width)
        gate_part = jnp.einsum(
            "rd,fd->rf", part_rows, expert_gate, preferred_element_type=jnp.float32
        )
        up_part = jnp.einsum("rd,fd->rf", part_rows, expert_up, preferred_element_type=jnp.float32)
        halves.append((jax.nn.silu(gate_part) * up_part).astype(jnp.bfloat16))
    hidden_units = jnp.concatenate(halves, axis=0)
    joined = lax.all_gather(hidden_units, "head", axis=1, tiled=True)
    partial_value = (
        jnp.dot(joined, expert_down, preferred_element_type=jnp.float32)
        .astype(jnp.bfloat16)
        .reshape(2, pairs, EXP, MOST, share_width)
    )
    pair_sum = (
        partial_value[0].astype(jnp.float32)
        + lax.ppermute(partial_value[1], "core", swap).astype(jnp.float32)
    ).astype(jnp.bfloat16)
    outgoing = pair_sum.transpose(1, 0, 2, 3).reshape(EXP * pairs, MOST, share_width)
    returned = lax.all_to_all(outgoing, ("g", "q"), split_axis=0, concat_axis=0, tiled=True)
    summed = jnp.sum(returned.astype(jnp.float32).reshape(EXP, pairs, MOST, share_width), axis=1)
    mixture = jnp.einsum("est,esd->td", weighted, summed, precision=highest)
    return (hidden_share + mixture).astype(jnp.bfloat16)


def solution(mesh):
    ctx_count = mesh.shape["ctx"]
    head_count = mesh.shape["head"]
    split = Mesh(
        mesh.devices.reshape(EXP, ctx_count // EXP // 2, 2, head_count), ("g", "q", "core", "head")
    )
    ctx = CTX
    return jax.shard_map(
        body,
        mesh=split,
        in_specs=(
            P(ctx, "head"),
            P(ctx, "head"),
            P(ctx, "head"),
            P(ctx, "head"),
            P(ctx, "head"),
            P("head"),
            P("head", ctx, None),
            P(ctx, None),
            P(),
            P(),
            P(ctx, None),
            P(ctx + ("head",), None),
            P(ctx + ("head",), None),
            P(ctx, "head"),
        ),
        out_specs=P(ctx, "head"),
        check_vma=False,
    )
```

```python
import jax
import jax.numpy as jnp
from jax import lax
from jax.sharding import Mesh, PartitionSpec as P

EXP = 8
MOST = 10
CTX = ("g", "q", "core")


epsilon = 1e-06
highest = lax.Precision.HIGHEST


def pack_state(factor, state):
    heads, dim, _ = state.shape
    extra = jnp.broadcast_to(factor[:, None, None], (heads, 8, dim))
    return jnp.concatenate([state, extra], axis=1)


def unpack_state(packed):
    dim = packed.shape[-1]
    return packed[:, dim, 0], packed[:, :dim, :]


def prefix_scan(factor, state, axis, count):
    place = lax.axis_index(axis)

    def shift(value, distance):
        return lax.ppermute(value, axis, [(i, i + distance) for i in range(count - distance)])

    identity = pack_state(jnp.ones_like(factor), jnp.zeros_like(state))
    current = jnp.where(place >= 1, shift(pack_state(factor, state), 1), identity)
    distance = 1
    while distance < count:
        earlier_factor, earlier_state = unpack_state(shift(current, distance))
        later_factor, later_state = unpack_state(current)
        joined = pack_state(
            earlier_factor * later_factor,
            later_factor[:, None, None] * earlier_state + later_state,
        )
        current = jnp.where(place >= distance, joined, current)
        distance *= 2
    return unpack_state(current)[1]


def body(
    queries,
    key_heads,
    value_heads,
    gate_logits,
    log_decay,
    attn_gain,
    out_weight,
    residual,
    norm_gain,
    router_weight,
    expert_ids,
    expert_gate,
    expert_up,
    expert_down,
):
    ctx_count = lax.axis_size(CTX)
    head_count = lax.axis_size("head")
    head_index = lax.axis_index("head")
    tok_rows = queries.shape[0]
    local_heads = log_decay.shape[1]
    head_dim = queries.shape[1] // local_heads
    model_width = residual.shape[1]
    share_width = model_width // head_count
    query_blocks = queries.reshape(tok_rows, local_heads, head_dim)
    key_blocks = key_heads.reshape(tok_rows, local_heads, head_dim)
    value_blocks = value_heads.reshape(tok_rows, local_heads, head_dim)
    cumulative = jnp.cumsum(log_decay, axis=0)
    block_total = cumulative[-1]
    keys_decayed = (
        key_blocks.astype(jnp.float32) * jnp.exp(block_total[None, :] - cumulative)[:, :, None]
    ).astype(jnp.bfloat16)
    local_state = jnp.einsum(
        "thd,the->hde", keys_decayed, value_blocks, preferred_element_type=jnp.float32
    )
    core = lax.axis_index("core")
    swap = [(0, 1), (1, 0)]
    factor = jnp.exp(block_total)
    partner_factor, partner_state = unpack_state(
        lax.ppermute(pack_state(factor, local_state), "core", swap)
    )
    first_factor = jnp.where(core == 0, factor, partner_factor)
    first_state = jnp.where(core == 0, local_state, partner_state)
    second_factor = jnp.where(core == 0, partner_factor, factor)
    second_state = jnp.where(core == 0, partner_state, local_state)
    chip_factor = first_factor * second_factor
    chip_state = second_factor[:, None, None] * first_state + second_state
    half = local_heads // 2
    half_factor = jnp.where(core == 0, chip_factor[:half], chip_factor[half:])
    half_state = jnp.where(core == 0, chip_state[:half], chip_state[half:])
    mine = prefix_scan(half_factor, half_state, ("g", "q"), ctx_count // 2)
    other = lax.ppermute(mine, "core", swap)
    chip_entering = jnp.concatenate(
        [jnp.where(core == 0, mine, other), jnp.where(core == 0, other, mine)], axis=0
    )
    entering = jnp.where(
        core == 0, chip_entering, first_factor[:, None, None] * chip_entering + first_state
    )
    sequence_offsets = jnp.arange(tok_rows)
    causal = (sequence_offsets[:, None] >= sequence_offsets[None, :])[None, :, :]
    cum_heads = cumulative.T
    decay_gaps = jnp.where(causal, cum_heads[:, :, None] - cum_heads[:, None, :], 0.0)
    scores = jnp.einsum(
        "thd,shd->hts", query_blocks, key_blocks, preferred_element_type=jnp.float32
    )
    attn_probs = jnp.where(causal, scores * jnp.exp(decay_gaps), 0.0).astype(jnp.bfloat16)
    within = jnp.einsum(
        "hts,shd->thd", attn_probs, value_blocks, preferred_element_type=jnp.float32
    )
    carried = jnp.einsum(
        "thd,hde->the", query_blocks.astype(jnp.float32), entering, precision=highest
    )
    attended = within + carried * jnp.exp(cumulative)[:, :, None]
    rms_scale = lax.rsqrt(jnp.mean(attended * attended, axis=-1, keepdims=True) + epsilon)
    gate_open = jax.nn.sigmoid(
        gate_logits.astype(jnp.float32).reshape(tok_rows, local_heads, head_dim)
    )
    attn_mixed = (
        attended * rms_scale * attn_gain.reshape(local_heads, head_dim) * gate_open
    ).astype(jnp.bfloat16)
    half_width = share_width // 2
    split_weight = out_weight.reshape(local_heads, -1, head_count, 2, half_width)
    mine = jnp.where(core == 0, split_weight[:, :, :, 0], split_weight[:, :, :, 1])
    theirs = jnp.where(core == 0, split_weight[:, :, :, 1], split_weight[:, :, :, 0])
    received = lax.ppermute(theirs, "core", swap)
    pair_rows = jnp.concatenate(
        [jnp.where(core == 0, mine, received), jnp.where(core == 0, received, mine)], axis=1
    )
    row_whole = lax.all_gather(pair_rows, ("g", "q"), axis=1, tiled=True)
    partner_mixed = lax.ppermute(attn_mixed, "core", swap)
    both_mixed = jnp.concatenate(
        [jnp.where(core == 0, attn_mixed, partner_mixed), jnp.where(core == 0, partner_mixed, attn_mixed)],
        axis=0,
    )
    partial_sum = jnp.einsum(
        "thr,hrqd->tqd", both_mixed, row_whole, preferred_element_type=jnp.float32
    )
    scattered = lax.psum_scatter(
        partial_sum.astype(jnp.bfloat16), "head", scatter_dimension=1, tiled=True
    ).reshape(2, tok_rows, half_width)
    own_rows = jnp.where(core == 0, scattered[0], scattered[1])
    other_rows = lax.ppermute(jnp.where(core == 0, scattered[1], scattered[0]), "core", swap)
    projected = jnp.concatenate(
        [jnp.where(core == 0, own_rows, other_rows), jnp.where(core == 0, other_rows, own_rows)],
        axis=1,
    ).astype(jnp.float32)
    share_start = head_index * share_width
    residual_share = lax.dynamic_slice_in_dim(residual, share_start, share_width, 1)
    gain_share = lax.dynamic_slice_in_dim(norm_gain, share_start, share_width, 0)
    router_share = lax.dynamic_slice_in_dim(router_weight, share_start, share_width, 0)
    hidden_share = residual_share.astype(jnp.float32) + projected
    router_part = jnp.dot(
        hidden_share * gain_share[None, :],
        router_share.astype(jnp.float32),
        precision=highest,
    )
    square_part = jnp.sum(hidden_share * hidden_share, axis=-1, keepdims=True)
    stats = lax.psum(jnp.concatenate([square_part, router_part], axis=1), "head")
    row_scale = lax.rsqrt(stats[:, :1] / model_width + epsilon)
    logits = stats[:, 1:] * row_scale
    normed_share = (hidden_share * row_scale * gain_share[None, :]).astype(jnp.bfloat16)
    columns = jnp.arange(router_weight.shape[1], dtype=jnp.int32)
    picked = jnp.sum(
        jnp.where(columns[None, None, :] == expert_ids[:, :, None], logits[:, None, :], 0.0),
        axis=-1,
    )
    route_gates = jax.nn.sigmoid(picked - picked[:, ::-1])
    route_ids = expert_ids.reshape(-1)
    onehot = (route_ids[:, None] == jnp.arange(EXP, dtype=jnp.int32)[None, :]).astype(jnp.int32)
    before_count = jnp.cumsum(onehot, axis=0) - onehot
    slot_index = jnp.sum(before_count * onehot, axis=1)
    slot_range = jnp.arange(MOST, dtype=jnp.int32)
    placed = (onehot.T[:, None, :] == 1) & (slot_index[None, None, :] == slot_range[None, :, None])
    chooser = (
        jnp.sum(placed.reshape(EXP, MOST, tok_rows, 2).astype(jnp.float32), axis=3)
        .astype(jnp.bfloat16)
        .reshape(EXP * MOST, tok_rows)
    )
    weighted = jnp.sum(
        (placed.astype(jnp.float32) * route_gates.reshape(-1)[None, None, :]).reshape(
            EXP, MOST, tok_rows, 2
        ),
        axis=3,
    )
    group = ctx_count // EXP
    packed = (
        jnp.dot(chooser, normed_share, preferred_element_type=jnp.float32)
        .astype(jnp.bfloat16)
        .reshape(EXP, MOST, share_width)
    )
    by_group = lax.all_to_all(packed, "g", split_axis=0, concat_axis=0, tiled=True)
    wide = lax.all_gather(by_group.reshape(EXP * MOST, share_width), "head", axis=1, tiled=True)
    own_parity = lax.all_gather(wide, "q", axis=0, tiled=False)
    other_parity = lax.ppermute(own_parity, "core", swap)
    pairs = group // 2
    halves = []
    for part in (own_parity, other_parity):
        part_rows = part.reshape(-1, model_width)
        gate_part = jnp.einsum(
            "rd,fd->rf", part_rows, expert_gate, preferred_element_type=jnp.float32
        )
        up_part = jnp.einsum("rd,fd->rf", part_rows, expert_up, preferred_element_type=jnp.float32)
        halves.append((jax.nn.silu(gate_part) * up_part).astype(jnp.bfloat16))
    hidden_units = jnp.concatenate(halves, axis=0)
    joined = lax.all_gather(hidden_units, "head", axis=1, tiled=True)
    partial_value = (
        jnp.dot(joined, expert_down, preferred_element_type=jnp.float32)
        .astype(jnp.bfloat16)
        .reshape(2, pairs, EXP, MOST, share_width)
    )
    pair_sum = (
        partial_value[0].astype(jnp.float32)
        + lax.ppermute(partial_value[1], "core", swap).astype(jnp.float32)
    ).astype(jnp.bfloat16)
    outgoing = pair_sum.transpose(1, 0, 2, 3).reshape(EXP * pairs, MOST, share_width)
    returned = lax.all_to_all(outgoing, ("g", "q"), split_axis=0, concat_axis=0, tiled=True)
    summed = jnp.sum(returned.astype(jnp.float32).reshape(EXP, pairs, MOST, share_width), axis=1)
    mixture = jnp.einsum("est,esd->td", weighted, summed, precision=highest)
    return (hidden_share + mixture).astype(jnp.bfloat16)


def solution(mesh):
    ctx_count = mesh.shape["ctx"]
    head_count = mesh.shape["head"]
    split = Mesh(
        mesh.devices.reshape(EXP, ctx_count // EXP // 2, 2, head_count), ("g", "q", "core", "head")
    )
    ctx = CTX
    return jax.shard_map(
        body,
        mesh=split,
        in_specs=(
            P(ctx, "head"),
            P(ctx, "head"),
            P(ctx, "head"),
            P(ctx, "head"),
            P(ctx, "head"),
            P("head"),
            P("head", ctx, None),
            P(ctx, None),
            P(),
            P(),
            P(ctx, None),
            P(ctx + ("head",), None),
            P(ctx + ("head",), None),
            P(ctx, "head"),
        ),
        out_specs=P(ctx, "head"),
        check_vma=False,
    )
```

```python
import jax
import jax.numpy as jnp
from jax import lax
from jax.sharding import Mesh, PartitionSpec as P

EXP = 8
MOST = 10
CTX = ("g", "q", "core")


epsilon = 1e-06
highest = lax.Precision.HIGHEST


def pack_state(factor, state):
    heads, dim, _ = state.shape
    extra = jnp.broadcast_to(factor[:, None, None], (heads, 8, dim))
    return jnp.concatenate([state, extra], axis=1)


def unpack_state(packed):
    dim = packed.shape[-1]
    return packed[:, dim, 0], packed[:, :dim, :]


def prefix_scan(factor, state, axis, count):
    place = lax.axis_index(axis)

    def shift(value, distance):
        return lax.ppermute(value, axis, [(i, i + distance) for i in range(count - distance)])

    identity = pack_state(jnp.ones_like(factor), jnp.zeros_like(state))
    current = jnp.where(place >= 1, shift(pack_state(factor, state), 1), identity)
    distance = 1
    while distance < count:
        earlier_factor, earlier_state = unpack_state(shift(current, distance))
        later_factor, later_state = unpack_state(current)
        joined = pack_state(
            earlier_factor * later_factor,
            later_factor[:, None, None] * earlier_state + later_state,
        )
        current = jnp.where(place >= distance, joined, current)
        distance *= 2
    return unpack_state(current)[1]


def body(
    queries,
    key_heads,
    value_heads,
    gate_logits,
    log_decay,
    attn_gain,
    out_weight,
    residual,
    norm_gain,
    router_weight,
    expert_ids,
    expert_gate,
    expert_up,
    expert_down,
):
    ctx_count = lax.axis_size(CTX)
    head_count = lax.axis_size("head")
    head_index = lax.axis_index("head")
    tok_rows = queries.shape[0]
    local_heads = log_decay.shape[1]
    head_dim = queries.shape[1] // local_heads
    model_width = residual.shape[1]
    share_width = model_width // head_count
    query_blocks = queries.reshape(tok_rows, local_heads, head_dim)
    key_blocks = key_heads.reshape(tok_rows, local_heads, head_dim)
    value_blocks = value_heads.reshape(tok_rows, local_heads, head_dim)
    cumulative = jnp.cumsum(log_decay, axis=0)
    block_total = cumulative[-1]
    keys_decayed = (
        key_blocks.astype(jnp.float32) * jnp.exp(block_total[None, :] - cumulative)[:, :, None]
    ).astype(jnp.bfloat16)
    local_state = jnp.einsum(
        "thd,the->hde", keys_decayed, value_blocks, preferred_element_type=jnp.float32
    )
    core = lax.axis_index("core")
    swap = [(0, 1), (1, 0)]
    factor = jnp.exp(block_total)
    partner_factor, partner_state = unpack_state(
        lax.ppermute(pack_state(factor, local_state), "core", swap)
    )
    first_factor = jnp.where(core == 0, factor, partner_factor)
    first_state = jnp.where(core == 0, local_state, partner_state)
    second_factor = jnp.where(core == 0, partner_factor, factor)
    second_state = jnp.where(core == 0, partner_state, local_state)
    chip_factor = first_factor * second_factor
    chip_state = second_factor[:, None, None] * first_state + second_state
    half = local_heads // 2
    half_factor = jnp.where(core == 0, chip_factor[:half], chip_factor[half:])
    half_state = jnp.where(core == 0, chip_state[:half], chip_state[half:])
    mine = prefix_scan(half_factor, half_state, ("g", "q"), ctx_count // 2)
    other = lax.ppermute(mine, "core", swap)
    chip_entering = jnp.concatenate(
        [jnp.where(core == 0, mine, other), jnp.where(core == 0, other, mine)], axis=0
    )
    entering = jnp.where(
        core == 0, chip_entering, first_factor[:, None, None] * chip_entering + first_state
    )
    sequence_offsets = jnp.arange(tok_rows)
    causal = (sequence_offsets[:, None] >= sequence_offsets[None, :])[None, :, :]
    cum_heads = cumulative.T
    decay_gaps = jnp.where(causal, cum_heads[:, :, None] - cum_heads[:, None, :], 0.0)
    scores = jnp.einsum(
        "thd,shd->hts", query_blocks, key_blocks, preferred_element_type=jnp.float32
    )
    attn_probs = jnp.where(causal, scores * jnp.exp(decay_gaps), 0.0).astype(jnp.bfloat16)
    within = jnp.einsum(
        "hts,shd->thd", attn_probs, value_blocks, preferred_element_type=jnp.float32
    )
    carried = jnp.einsum(
        "thd,hde->the", query_blocks.astype(jnp.float32), entering, precision=highest
    )
    attended = within + carried * jnp.exp(cumulative)[:, :, None]
    rms_scale = lax.rsqrt(jnp.mean(attended * attended, axis=-1, keepdims=True) + epsilon)
    gate_open = jax.nn.sigmoid(
        gate_logits.astype(jnp.float32).reshape(tok_rows, local_heads, head_dim)
    )
    attn_mixed = (
        attended * rms_scale * attn_gain.reshape(local_heads, head_dim) * gate_open
    ).astype(jnp.bfloat16)
    half_width = share_width // 2
    split_weight = out_weight.reshape(local_heads, -1, head_count, 2, half_width)
    mine = jnp.where(core == 0, split_weight[:, :, :, 0], split_weight[:, :, :, 1])
    theirs = jnp.where(core == 0, split_weight[:, :, :, 1], split_weight[:, :, :, 0])
    received = lax.ppermute(theirs, "core", swap)
    pair_rows = jnp.concatenate(
        [jnp.where(core == 0, mine, received), jnp.where(core == 0, received, mine)], axis=1
    )
    row_whole = lax.all_gather(pair_rows, ("g", "q"), axis=1, tiled=True)
    partner_mixed = lax.ppermute(attn_mixed, "core", swap)
    both_mixed = jnp.concatenate(
        [jnp.where(core == 0, attn_mixed, partner_mixed), jnp.where(core == 0, partner_mixed, attn_mixed)],
        axis=0,
    )
    partial_sum = jnp.einsum(
        "thr,hrqd->tqd", both_mixed, row_whole, preferred_element_type=jnp.float32
    )
    scattered = lax.psum_scatter(
        partial_sum.astype(jnp.bfloat16), "head", scatter_dimension=1, tiled=True
    ).reshape(2, tok_rows, half_width)
    own_rows = jnp.where(core == 0, scattered[0], scattered[1])
    other_rows = lax.ppermute(jnp.where(core == 0, scattered[1], scattered[0]), "core", swap)
    projected = jnp.concatenate(
        [jnp.where(core == 0, own_rows, other_rows), jnp.where(core == 0, other_rows, own_rows)],
        axis=1,
    ).astype(jnp.float32)
    share_start = head_index * share_width
    residual_share = lax.dynamic_slice_in_dim(residual, share_start, share_width, 1)
    gain_share = lax.dynamic_slice_in_dim(norm_gain, share_start, share_width, 0)
    router_share = lax.dynamic_slice_in_dim(router_weight, share_start, share_width, 0)
    hidden_share = residual_share.astype(jnp.float32) + projected
    router_part = jnp.dot(
        hidden_share * gain_share[None, :],
        router_share.astype(jnp.float32),
        precision=highest,
    )
    square_part = jnp.sum(hidden_share * hidden_share, axis=-1, keepdims=True)
    stats = lax.psum(jnp.concatenate([square_part, router_part], axis=1), "head")
    row_scale = lax.rsqrt(stats[:, :1] / model_width + epsilon)
    logits = stats[:, 1:] * row_scale
    normed_share = (hidden_share * row_scale * gain_share[None, :]).astype(jnp.bfloat16)
    columns = jnp.arange(router_weight.shape[1], dtype=jnp.int32)
    picked = jnp.sum(
        jnp.where(columns[None, None, :] == expert_ids[:, :, None], logits[:, None, :], 0.0),
        axis=-1,
    )
    route_gates = jax.nn.sigmoid(picked - picked[:, ::-1])
    route_ids = expert_ids.reshape(-1)
    onehot = (route_ids[:, None] == jnp.arange(EXP, dtype=jnp.int32)[None, :]).astype(jnp.int32)
    before_count = jnp.cumsum(onehot, axis=0) - onehot
    slot_index = jnp.sum(before_count * onehot, axis=1)
    slot_range = jnp.arange(MOST, dtype=jnp.int32)
    placed = (onehot.T[:, None, :] == 1) & (slot_index[None, None, :] == slot_range[None, :, None])
    chooser = (
        jnp.sum(placed.reshape(EXP, MOST, tok_rows, 2).astype(jnp.float32), axis=3)
        .astype(jnp.bfloat16)
        .reshape(EXP * MOST, tok_rows)
    )
    weighted = jnp.sum(
        (placed.astype(jnp.float32) * route_gates.reshape(-1)[None, None, :]).reshape(
            EXP, MOST, tok_rows, 2
        ),
        axis=3,
    )
    group = ctx_count // EXP
    packed = (
        jnp.dot(chooser, normed_share, preferred_element_type=jnp.float32)
        .astype(jnp.bfloat16)
        .reshape(EXP, MOST, share_width)
    )
    by_group = lax.all_to_all(packed, "g", split_axis=0, concat_axis=0, tiled=True)
    wide = lax.all_gather(by_group.reshape(EXP * MOST, share_width), "head", axis=1, tiled=True)
    q_count = lax.axis_size("q")
    q_place = lax.axis_index("q")
    shifted = [wide] + [
        lax.ppermute(wide, "q", [(i, (i + s) % q_count) for i in range(q_count)])
        for s in range(1, q_count)
    ]
    order = (q_place - jnp.arange(q_count)) % q_count
    own_parity = jnp.take(jnp.stack(shifted), order, axis=0)
    other_parity = lax.ppermute(own_parity, "core", swap)
    pairs = group // 2
    halves = []
    for part in (own_parity, other_parity):
        part_rows = part.reshape(-1, model_width)
        gate_part = jnp.einsum(
            "rd,fd->rf", part_rows, expert_gate, preferred_element_type=jnp.float32
        )
        up_part = jnp.einsum("rd,fd->rf", part_rows, expert_up, preferred_element_type=jnp.float32)
        halves.append((jax.nn.silu(gate_part) * up_part).astype(jnp.bfloat16))
    hidden_units = jnp.concatenate(halves, axis=0)
    joined = lax.all_gather(hidden_units, "head", axis=1, tiled=True)
    partial_value = (
        jnp.dot(joined, expert_down, preferred_element_type=jnp.float32)
        .astype(jnp.bfloat16)
        .reshape(2, pairs, EXP, MOST, share_width)
    )
    pair_sum = (
        partial_value[0].astype(jnp.float32)
        + lax.ppermute(partial_value[1], "core", swap).astype(jnp.float32)
    ).astype(jnp.bfloat16)
    outgoing = pair_sum.transpose(1, 0, 2, 3).reshape(EXP * pairs, MOST, share_width)
    returned = lax.all_to_all(outgoing, ("g", "q"), split_axis=0, concat_axis=0, tiled=True)
    summed = jnp.sum(returned.astype(jnp.float32).reshape(EXP, pairs, MOST, share_width), axis=1)
    mixture = jnp.einsum("est,esd->td", weighted, summed, precision=highest)
    return (hidden_share + mixture).astype(jnp.bfloat16)


def solution(mesh):
    ctx_count = mesh.shape["ctx"]
    head_count = mesh.shape["head"]
    split = Mesh(
        mesh.devices.reshape(EXP, ctx_count // EXP // 2, 2, head_count), ("g", "q", "core", "head")
    )
    ctx = CTX
    return jax.shard_map(
        body,
        mesh=split,
        in_specs=(
            P(ctx, "head"),
            P(ctx, "head"),
            P(ctx, "head"),
            P(ctx, "head"),
            P(ctx, "head"),
            P("head"),
            P("head", ctx, None),
            P(ctx, None),
            P(),
            P(),
            P(ctx, None),
            P(ctx + ("head",), None),
            P(ctx + ("head",), None),
            P(ctx, "head"),
        ),
        out_specs=P(ctx, "head"),
        check_vma=False,
    )
```
